32 devices in a mesh: bond: 4 (over x, core), rows: 8 (over z, y).
Axes of the slice: x: 2, y: 2, z: 4, core: 2. Of those that a mesh axis runs over, the one named last changes fastest.
Arguments:
- amps_left: float32 [2, 4096, 12288], P(None, 'rows', 'bond'), may hold values from -0.0390625 to 0.0390625
- amps_right: float32 [2, 512, 12288], P(None, 'rows', 'bond'), may hold values from -6 to 6
- axis_order: int32 [21], replicated, may hold values from 0 to 20, as said below
Outputs:
- regrouped: float32 [2, 4096, 512], P(None, 'rows', 'bond')
The draws below stay inside these ranges and needn't reach their ends.
Inputs may be any that keep to these rules, and one draw needn't show every extreme that they name: axis_order is a permutation. For every bit p of the result among its highest log2 * 8 row bits and its highest log2 * 4 column bits, axis_order[p] is none of: the highest log2 * 8 row bits of the product, the log2 * 4 row bits just below them, the highest log2 * 4 column bits of the product. Bits count from the least significant bit of the flat index, columns first.
All inputs are finite; a program needn't handle non-finite values.
Results may differ from the reference program's by a relative error of at most 0.00007.
Values sent between devices are 32-bit elements; how exact they have to be, the bound alone decides.
No kernel may reach another device: no remote copies, remote signals or barrier semaphores. Data moves between devices by JAX's collectives and lax.ppermute only.
A program may use at most 128 MiB of HBM per device.

```python
import jax
import jax.numpy as jnp
from jax import lax

ROW_BITS = 12
COL_BITS = 9
BOND_DIM = 12288
ROWS_ALL = 4096
COLUMNS = 512
N_BOND = 4
N_ROWS = 8


def draw_axis_order(key, part):
    total_bits = ROW_BITS + COL_BITS
    row_devbits = N_ROWS.bit_length() - 1
    bond_devbits = N_BOND.bit_length() - 1
    guarded = list(range(total_bits - row_devbits - bond_devbits, total_bits)) + list(range(COL_BITS - bond_devbits, COL_BITS))
    others = [value for value in range(total_bits) if value not in guarded]
    out_dev = list(range(total_bits - row_devbits, total_bits)) + list(range(COL_BITS - bond_devbits, COL_BITS))
    out_local = [value for value in range(total_bits) if value not in out_dev]
    first_key = jax.random.fold_in(key, 11)
    second_key = jax.random.fold_in(key, 23)
    shuffled = jax.random.permutation(first_key, jnp.array(others, dtype=jnp.int32))
    count = len(out_dev)
    rest = jnp.concatenate([shuffled[count:], jnp.array(guarded, dtype=jnp.int32)])
    rest = jax.random.permutation(second_key, rest)
    order = jnp.zeros((total_bits,), jnp.int32)
    order = order.at[jnp.array(out_dev, dtype=jnp.int32)].set(shuffled[:count])
    order = order.at[jnp.array(out_local, dtype=jnp.int32)].set(rest)
    return order


def steps_of(rng, shape, shards, least, largest):
    level, own = 1.0, jax.random.fold_in(rng, 6)
    for dim, blocks in shards:
        heights = jnp.exp(jax.random.uniform(jax.random.fold_in(own, dim), (blocks,), jnp.float32, least / len(shards), largest / len(shards)))
        level = level * jnp.repeat(heights, shape[dim] // blocks).reshape([-1 if axis == dim else 1 for axis in range(len(shape))])
    return level


def normal_values(rng, dims, scale, bound, split=(), kind=jnp.bfloat16):
    result = scale * jax.random.normal(rng, dims, jnp.float32)
    if split:
        result = result * steps_of(rng, dims, split, -0.22, 0.18)
    return jnp.clip(result, -bound, bound).astype(kind)


def setup_inputs(seed: int = 0) -> dict:
    key_list = jax.random.split(jax.random.key(seed), 4)
    amps_left = normal_values(key_list[0], (2, ROWS_ALL, BOND_DIM), (2 * BOND_DIM) ** -0.5, 0.0390625, ((1, 8), (2, 4)), jnp.float32)
    amps_right = normal_values(key_list[1], (2, COLUMNS, BOND_DIM), 1.0, 6.0, ((1, 8), (2, 4)), jnp.float32)
    axis_order = draw_axis_order(jax.random.fold_in(key_list[3], 71), 0)
    return dict(amps_left=amps_left, amps_right=amps_right, axis_order=axis_order)


def cross_dot(left, right):
    return lax.dot_general(left, right, (((1,), (1,)), ((), ())), precision=lax.Precision.HIGHEST, preferred_element_type=jnp.float32)


def reference(amps_left, amps_right, axis_order):
    real_part = cross_dot(amps_left[0], amps_right[0]) - cross_dot(amps_left[1], amps_right[1])
    imag_part = cross_dot(amps_left[0], amps_right[1]) + cross_dot(amps_left[1], amps_right[0])
    product = jnp.stack([real_part, imag_part]).reshape(2, -1)
    total_bits = ROW_BITS + COL_BITS
    target = jnp.arange(2 ** total_bits, dtype=jnp.int32)
    source = jnp.zeros_like(target)
    for position in range(total_bits):
        source = source + jnp.left_shift(jnp.right_shift(target, position) & 1, axis_order[position].astype(jnp.int32))
    return jnp.take(product, source, axis=1).reshape(2, 2 ** ROW_BITS, 2 ** COL_BITS)
```

```python
import jax
import jax.numpy as jnp
from jax import lax
from jax.sharding import PartitionSpec as P

ROW_BITS = 12
COL_BITS = 9


def cross_dot(left, right):
    return lax.dot_general(
        left,
        right,
        (((1,), (1,)), ((), ())),
        precision=lax.Precision.HIGHEST,
        preferred_element_type=jnp.float32,
    )


def rank_within(keys, member):
    below = (keys[None, :] < keys[:, None]) & member[None, :]
    return jnp.sum(below.astype(jnp.int32), axis=1)


def perm_matrix(new_pos, nbits):
    old = jnp.arange(2**nbits, dtype=jnp.int32)
    moved = jnp.zeros_like(old)
    for bit_num in range(nbits):
        moved = moved + jnp.left_shift(jnp.right_shift(old, bit_num) & 1, new_pos[bit_num])
    return (old[:, None] == moved[None, :]).astype(jnp.float32)


def permute_rows(block, new_pos, nbits):
    mat = perm_matrix(new_pos, nbits)
    return jnp.einsum("no,pol->pnl", mat, block, precision=lax.Precision.HIGHEST)


def permute_lanes(block, new_pos, nbits):
    mat = perm_matrix(new_pos, nbits)
    return jnp.einsum("no,pro->prn", mat, block, precision=lax.Precision.HIGHEST)


def cross_swap(block, m, rbits, cbits):
    def branch(k):
        def run(x):
            planes = x.shape[0]
            x = x.reshape(planes, 2 ** (rbits - k), 2**k, 2**k, 2 ** (cbits - k))
            x = jnp.transpose(x, (0, 1, 3, 2, 4))
            return x.reshape(planes, 2**rbits, 2**cbits)

        return run

    return lax.switch(m, [branch(k) for k in range(min(rbits, cbits) + 1)], block)


def bit_permute(block, src):
    rbits = block.shape[1].bit_length() - 1
    cbits = block.shape[2].bit_length() - 1
    total = rbits + cbits
    dest_of = jnp.zeros((total,), jnp.int32).at[src].set(jnp.arange(total, dtype=jnp.int32))
    pos = jnp.arange(total, dtype=jnp.int32)
    is_lane = pos < cbits
    goes_lane = dest_of < cbits
    lane_stay = is_lane & goes_lane
    lane_go = is_lane & ~goes_lane
    row_stay = ~is_lane & ~goes_lane
    row_go = ~is_lane & goes_lane
    m = jnp.sum(row_go.astype(jnp.int32))
    r_lane_stay = rank_within(dest_of, lane_stay)
    r_lane_go = rank_within(dest_of, lane_go)
    r_row_stay = rank_within(dest_of, row_stay)
    r_row_go = rank_within(dest_of, row_go)
    first_rows = jnp.where(row_go, r_row_go, m + r_row_stay)[cbits:]
    first_lanes = jnp.where(lane_go, cbits - m + r_lane_go, r_lane_stay)[:cbits]
    block = permute_rows(block, first_rows, rbits)
    block = permute_lanes(block, first_lanes, cbits)
    block = cross_swap(block, m, rbits, cbits)
    lane_src_pos = jnp.where(lane_stay, r_lane_stay, cbits - m + r_row_go)
    lane_members = lane_stay | row_go
    row_src_pos = jnp.where(lane_go, r_lane_go, m + r_row_stay)
    row_members = lane_go | row_stay
    second_lanes = jnp.zeros((cbits,), jnp.int32).at[
        jnp.where(lane_members, lane_src_pos, cbits)
    ].set(dest_of, mode="drop")
    second_rows = jnp.zeros((rbits,), jnp.int32).at[
        jnp.where(row_members, row_src_pos, rbits)
    ].set(dest_of - cbits, mode="drop")
    block = permute_rows(block, second_rows, rbits)
    block = permute_lanes(block, second_lanes, cbits)
    return block


def regroup(block, axis_order):
    nrows = lax.axis_size("rows")
    nbond = lax.axis_size("bond")
    row_devbits = nrows.bit_length() - 1
    bond_devbits = nbond.bit_length() - 1
    total_bits = ROW_BITS + COL_BITS
    lrows = ROW_BITS - row_devbits
    lcols = COL_BITS - bond_devbits
    nlocal = lrows + lcols
    devbits = row_devbits + bond_devbits
    local_of = []
    for bit in range(total_bits):
        if bit < lcols:
            local_of.append(bit)
        elif COL_BITS <= bit < COL_BITS + lrows:
            local_of.append(bit - COL_BITS + lcols)
        else:
            local_of.append(-1)
    local_of = jnp.array(local_of, dtype=jnp.int32)
    out_dev = [COL_BITS + lrows + k for k in range(row_devbits)] + [
        lcols + k for k in range(bond_devbits)
    ]
    dev_src = local_of[axis_order[jnp.array(out_dev, dtype=jnp.int32)]]
    pos = jnp.arange(nlocal, dtype=jnp.int32)
    is_dev = jnp.any(pos[:, None] == dev_src[None, :], axis=1)
    keep = ~is_dev
    keep_rank = rank_within(pos, keep)
    src_a = jnp.zeros((nlocal,), jnp.int32).at[
        jnp.where(keep, keep_rank, nlocal)
    ].set(pos, mode="drop")
    src_a = src_a.at[nlocal - devbits + jnp.arange(devbits)].set(dev_src)
    block = bit_permute(block, src_a)
    planes = block.shape[0]
    devices = nrows * nbond
    block = block.reshape(planes, devices, -1)
    block = lax.all_to_all(block, ("bond", "rows"), split_axis=1, concat_axis=1, tiled=True)
    block = block.reshape(planes, 2**lrows, 2**lcols)
    src_dev_bits = [COL_BITS + lrows + k for k in range(row_devbits)] + [
        lcols + k for k in range(bond_devbits)
    ]
    pos_w = jnp.full((total_bits,), -1, jnp.int32)
    within = jnp.zeros((nlocal,), jnp.int32).at[jnp.where(keep, keep_rank, nlocal)].set(
        pos, mode="drop"
    )
    prod_of_local = jnp.array(
        [b for b in range(total_bits) if b < lcols]
        + [b for b in range(COL_BITS, COL_BITS + lrows)],
        dtype=jnp.int32,
    )
    pos_w = pos_w.at[prod_of_local[within[: nlocal - devbits]]].set(
        jnp.arange(nlocal - devbits, dtype=jnp.int32)
    )
    pos_w = pos_w.at[jnp.array(src_dev_bits, dtype=jnp.int32)].set(
        nlocal - devbits + jnp.arange(devbits, dtype=jnp.int32)
    )
    out_local = [b for b in range(lcols)] + [COL_BITS + k for k in range(lrows)]
    src_c = pos_w[axis_order[jnp.array(out_local, dtype=jnp.int32)]]
    return bit_permute(block, src_c)


def per_device(amps_left, amps_right, axis_order):
    gathered = lax.all_gather(amps_right, "rows", axis=1, tiled=True)
    real_part = cross_dot(amps_left[0], gathered[0]) - cross_dot(amps_left[1], gathered[1])
    imag_part = cross_dot(amps_left[0], gathered[1]) + cross_dot(amps_left[1], gathered[0])
    partial_sums = jnp.stack([real_part, imag_part])
    block = lax.psum_scatter(partial_sums, "bond", scatter_dimension=2, tiled=True)
    return regroup(block, axis_order)


def solution(mesh):
    placed = (P(None, "rows", "bond"), P(None, "rows", "bond"), P())
    return jax.shard_map(
        per_device, mesh=mesh, in_specs=placed, out_specs=P(None, "rows", "bond"), check_vma=False
    )
```

```python
import jax
import jax.numpy as jnp
from jax import lax
from jax.sharding import PartitionSpec as P

ROW_BITS = 12
COL_BITS = 9


def cross_dot(left, right):
    return lax.dot_general(
        left,
        right,
        (((1,), (1,)), ((), ())),
        precision=lax.Precision.HIGHEST,
        preferred_element_type=jnp.float32,
    )


def rank_within(keys, member):
    below = (keys[None, :] < keys[:, None]) & member[None, :]
    return jnp.sum(below.astype(jnp.int32), axis=1)


def perm_matrix(new_pos, nbits):
    old = jnp.arange(2**nbits, dtype=jnp.int32)
    moved = jnp.zeros_like(old)
    for bit_num in range(nbits):
        moved = moved + jnp.left_shift(jnp.right_shift(old, bit_num) & 1, new_pos[bit_num])
    return (old[:, None] == moved[None, :]).astype(jnp.float32)


def permute_rows(block, mat):
    return jnp.einsum("no,pol->pnl", mat, block, precision=lax.Precision.HIGHEST)


def permute_lanes(block, mat):
    return jnp.einsum("no,pro->prn", mat, block, precision=lax.Precision.HIGHEST)


def cross_swap(block, m, rbits, cbits):
    def branch(k):
        def run(x):
            planes = x.shape[0]
            x = x.reshape(planes, 2 ** (rbits - k), 2**k, 2**k, 2 ** (cbits - k))
            x = jnp.transpose(x, (0, 1, 3, 2, 4))
            return x.reshape(planes, 2**rbits, 2**cbits)

        return run

    return lax.switch(m, [branch(k) for k in range(min(rbits, cbits) + 1)], block)


def plan_permute(src, rbits, cbits):
    total = rbits + cbits
    dest_of = jnp.zeros((total,), jnp.int32).at[src].set(jnp.arange(total, dtype=jnp.int32))
    pos = jnp.arange(total, dtype=jnp.int32)
    is_lane = pos < cbits
    goes_lane = dest_of < cbits
    lane_stay = is_lane & goes_lane
    lane_go = is_lane & ~goes_lane
    row_stay = ~is_lane & ~goes_lane
    row_go = ~is_lane & goes_lane
    m = jnp.sum(row_go.astype(jnp.int32))
    r_lane_stay = rank_within(dest_of, lane_stay)
    r_lane_go = rank_within(dest_of, lane_go)
    r_row_stay = rank_within(dest_of, row_stay)
    r_row_go = rank_within(dest_of, row_go)
    first_rows = jnp.where(row_go, r_row_go, m + r_row_stay)[cbits:]
    first_lanes = jnp.where(lane_go, cbits - m + r_lane_go, r_lane_stay)[:cbits]
    lane_src_pos = jnp.where(lane_stay, r_lane_stay, cbits - m + r_row_go)
    lane_members = lane_stay | row_go
    row_src_pos = jnp.where(lane_go, r_lane_go, m + r_row_stay)
    row_members = lane_go | row_stay
    second_lanes = jnp.zeros((cbits,), jnp.int32).at[
        jnp.where(lane_members, lane_src_pos, cbits)
    ].set(dest_of, mode="drop")
    second_rows = jnp.zeros((rbits,), jnp.int32).at[
        jnp.where(row_members, row_src_pos, rbits)
    ].set(dest_of - cbits, mode="drop")
    mats = (
        perm_matrix(first_rows, rbits),
        perm_matrix(first_lanes, cbits),
        perm_matrix(second_rows, rbits),
        perm_matrix(second_lanes, cbits),
    )
    return mats, m


def apply_permute(block, plan):
    (rows_a, lanes_a, rows_b, lanes_b), m = plan
    rbits = block.shape[1].bit_length() - 1
    cbits = block.shape[2].bit_length() - 1
    block = permute_rows(block, rows_a)
    block = permute_lanes(block, lanes_a)
    block = cross_swap(block, m, rbits, cbits)
    block = permute_rows(block, rows_b)
    return permute_lanes(block, lanes_b)


def make_plans(axis_order):
    nrows = lax.axis_size("rows")
    nbond = lax.axis_size("bond")
    row_devbits = nrows.bit_length() - 1
    bond_devbits = nbond.bit_length() - 1
    total_bits = ROW_BITS + COL_BITS
    lrows = ROW_BITS - row_devbits
    lcols = COL_BITS - bond_devbits
    nlocal = lrows + lcols
    devbits = row_devbits + bond_devbits
    local_of = []
    for bit in range(total_bits):
        if bit < lcols:
            local_of.append(bit)
        elif COL_BITS <= bit < COL_BITS + lrows:
            local_of.append(bit - COL_BITS + lcols)
        else:
            local_of.append(-1)
    local_of = jnp.array(local_of, dtype=jnp.int32)
    out_dev = [COL_BITS + lrows + k for k in range(row_devbits)] + [
        lcols + k for k in range(bond_devbits)
    ]
    dev_src = local_of[axis_order[jnp.array(out_dev, dtype=jnp.int32)]]
    pos = jnp.arange(nlocal, dtype=jnp.int32)
    is_dev = jnp.any(pos[:, None] == dev_src[None, :], axis=1)
    keep = ~is_dev
    keep_rank = rank_within(pos, keep)
    src_a = jnp.zeros((nlocal,), jnp.int32).at[
        jnp.where(keep, keep_rank, nlocal)
    ].set(pos, mode="drop")
    src_a = src_a.at[nlocal - devbits + jnp.arange(devbits)].set(dev_src)
    plan_a = plan_permute(src_a, lrows, lcols)
    src_dev_bits = [COL_BITS + lrows + k for k in range(row_devbits)] + [
        lcols + k for k in range(bond_devbits)
    ]
    pos_w = jnp.full((total_bits,), -1, jnp.int32)
    within = jnp.zeros((nlocal,), jnp.int32).at[jnp.where(keep, keep_rank, nlocal)].set(
        pos, mode="drop"
    )
    prod_of_local = jnp.array(
        [b for b in range(total_bits) if b < lcols]
        + [b for b in range(COL_BITS, COL_BITS + lrows)],
        dtype=jnp.int32,
    )
    pos_w = pos_w.at[prod_of_local[within[: nlocal - devbits]]].set(
        jnp.arange(nlocal - devbits, dtype=jnp.int32)
    )
    pos_w = pos_w.at[jnp.array(src_dev_bits, dtype=jnp.int32)].set(
        nlocal - devbits + jnp.arange(devbits, dtype=jnp.int32)
    )
    out_local = [b for b in range(lcols)] + [COL_BITS + k for k in range(lrows)]
    src_c = pos_w[axis_order[jnp.array(out_local, dtype=jnp.int32)]]
    plan_c = plan_permute(src_c, lrows, lcols)
    return plan_a, plan_c


def regroup(block, plans):
    plan_a, plan_c = plans
    planes, nrow, ncol = block.shape
    devices = lax.axis_size("rows") * lax.axis_size("bond")
    block = apply_permute(block, plan_a)
    block = block.reshape(planes, devices, -1)
    block = lax.all_to_all(block, ("bond", "rows"), split_axis=1, concat_axis=1, tiled=True)
    block = block.reshape(planes, nrow, ncol)
    return apply_permute(block, plan_c)


def per_device(amps_left, amps_right, axis_order):
    plans = make_plans(axis_order)
    nchunks = 4
    width = amps_right.shape[2] // nchunks
    real_part = imag_part = None
    for k in range(nchunks):
        cut = slice(k * width, (k + 1) * width)
        piece = lax.all_gather(amps_right[:, :, cut], "rows", axis=1, tiled=True)
        if k == 0:
            piece, plans = lax.optimization_barrier((piece, plans))
        left = amps_left[:, :, cut]
        real_k = cross_dot(left[0], piece[0]) - cross_dot(left[1], piece[1])
        imag_k = cross_dot(left[0], piece[1]) + cross_dot(left[1], piece[0])
        if k == 0:
            real_part, imag_part = real_k, imag_k
        else:
            real_part, imag_part = real_part + real_k, imag_part + imag_k
    partial_sums = jnp.stack([real_part, imag_part])
    block = lax.psum_scatter(partial_sums, "bond", scatter_dimension=2, tiled=True)
    return regroup(block, plans)


def solution(mesh):
    placed = (P(None, "rows", "bond"), P(None, "rows", "bond"), P())
    return jax.shard_map(
        per_device, mesh=mesh, in_specs=placed, out_specs=P(None, "rows", "bond"), check_vma=False
    )
```

```python
import jax
import jax.numpy as jnp
from jax import lax
from jax.sharding import PartitionSpec as P

ROW_BITS = 12
COL_BITS = 9


def cross_dot(left, right):
    return lax.dot_general(
        left,
        right,
        (((1,), (1,)), ((), ())),
        precision=lax.Precision.HIGH,
        preferred_element_type=jnp.float32,
    )


def rank_within(keys, member):
    below = (keys[None, :] < keys[:, None]) & member[None, :]
    return jnp.sum(below.astype(jnp.int32), axis=1)


def perm_matrix(new_pos, nbits):
    old = jnp.arange(2**nbits, dtype=jnp.int32)
    moved = jnp.zeros_like(old)
    for bit_num in range(nbits):
        moved = moved + jnp.left_shift(jnp.right_shift(old, bit_num) & 1, new_pos[bit_num])
    return (old[:, None] == moved[None, :]).astype(jnp.float32)


def permute_rows(block, mat):
    return jnp.einsum("no,pol->pnl", mat, block, precision=lax.Precision.HIGHEST)


def permute_lanes(block, mat):
    return jnp.einsum("no,pro->prn", mat, block, precision=lax.Precision.HIGHEST)


def cross_swap(block, m, rbits, cbits):
    def branch(k):
        def run(x):
            planes = x.shape[0]
            x = x.reshape(planes, 2 ** (rbits - k), 2**k, 2**k, 2 ** (cbits - k))
            x = jnp.transpose(x, (0, 1, 3, 2, 4))
            return x.reshape(planes, 2**rbits, 2**cbits)

        return run

    return lax.switch(m, [branch(k) for k in range(min(rbits, cbits) + 1)], block)


def plan_permute(src, rbits, cbits):
    total = rbits + cbits
    dest_of = jnp.zeros((total,), jnp.int32).at[src].set(jnp.arange(total, dtype=jnp.int32))
    pos = jnp.arange(total, dtype=jnp.int32)
    is_lane = pos < cbits
    goes_lane = dest_of < cbits
    lane_stay = is_lane & goes_lane
    lane_go = is_lane & ~goes_lane
    row_stay = ~is_lane & ~goes_lane
    row_go = ~is_lane & goes_lane
    m = jnp.sum(row_go.astype(jnp.int32))
    r_lane_stay = rank_within(dest_of, lane_stay)
    r_lane_go = rank_within(dest_of, lane_go)
    r_row_stay = rank_within(dest_of, row_stay)
    r_row_go = rank_within(dest_of, row_go)
    first_rows = jnp.where(row_go, r_row_go, m + r_row_stay)[cbits:]
    first_lanes = jnp.where(lane_go, cbits - m + r_lane_go, r_lane_stay)[:cbits]
    lane_src_pos = jnp.where(lane_stay, r_lane_stay, cbits - m + r_row_go)
    lane_members = lane_stay | row_go
    row_src_pos = jnp.where(lane_go, r_lane_go, m + r_row_stay)
    row_members = lane_go | row_stay
    second_lanes = jnp.zeros((cbits,), jnp.int32).at[
        jnp.where(lane_members, lane_src_pos, cbits)
    ].set(dest_of, mode="drop")
    second_rows = jnp.zeros((rbits,), jnp.int32).at[
        jnp.where(row_members, row_src_pos, rbits)
    ].set(dest_of - cbits, mode="drop")
    mats = (
        perm_matrix(first_rows, rbits),
        perm_matrix(first_lanes, cbits),
        perm_matrix(second_rows, rbits),
        perm_matrix(second_lanes, cbits),
    )
    return mats, m


def apply_permute(block, plan):
    (rows_a, lanes_a, rows_b, lanes_b), m = plan
    rbits = block.shape[1].bit_length() - 1
    cbits = block.shape[2].bit_length() - 1
    block = permute_rows(block, rows_a)
    block = permute_lanes(block, lanes_a)
    block = cross_swap(block, m, rbits, cbits)
    block = permute_rows(block, rows_b)
    return permute_lanes(block, lanes_b)


def make_plans(axis_order):
    nrows = lax.axis_size("rows")
    nbond = lax.axis_size("bond")
    row_devbits = nrows.bit_length() - 1
    bond_devbits = nbond.bit_length() - 1
    total_bits = ROW_BITS + COL_BITS
    lrows = ROW_BITS - row_devbits
    lcols = COL_BITS - bond_devbits
    nlocal = lrows + lcols
    devbits = row_devbits + bond_devbits
    local_of = []
    for bit in range(total_bits):
        if bit < lcols:
            local_of.append(bit)
        elif COL_BITS <= bit < COL_BITS + lrows:
            local_of.append(bit - COL_BITS + lcols)
        else:
            local_of.append(-1)
    local_of = jnp.array(local_of, dtype=jnp.int32)
    out_dev = [COL_BITS + lrows + k for k in range(row_devbits)] + [
        lcols + k for k in range(bond_devbits)
    ]
    dev_src = local_of[axis_order[jnp.array(out_dev, dtype=jnp.int32)]]
    pos = jnp.arange(nlocal, dtype=jnp.int32)
    is_dev = jnp.any(pos[:, None] == dev_src[None, :], axis=1)
    keep = ~is_dev
    keep_rank = rank_within(pos, keep)
    src_a = jnp.zeros((nlocal,), jnp.int32).at[
        jnp.where(keep, keep_rank, nlocal)
    ].set(pos, mode="drop")
    src_a = src_a.at[nlocal - devbits + jnp.arange(devbits)].set(dev_src)
    plan_a = plan_permute(src_a, lrows, lcols)
    src_dev_bits = [COL_BITS + lrows + k for k in range(row_devbits)] + [
        lcols + k for k in range(bond_devbits)
    ]
    pos_w = jnp.full((total_bits,), -1, jnp.int32)
    within = jnp.zeros((nlocal,), jnp.int32).at[jnp.where(keep, keep_rank, nlocal)].set(
        pos, mode="drop"
    )
    prod_of_local = jnp.array(
        [b for b in range(total_bits) if b < lcols]
        + [b for b in range(COL_BITS, COL_BITS + lrows)],
        dtype=jnp.int32,
    )
    pos_w = pos_w.at[prod_of_local[within[: nlocal - devbits]]].set(
        jnp.arange(nlocal - devbits, dtype=jnp.int32)
    )
    pos_w = pos_w.at[jnp.array(src_dev_bits, dtype=jnp.int32)].set(
        nlocal - devbits + jnp.arange(devbits, dtype=jnp.int32)
    )
    out_local = [b for b in range(lcols)] + [COL_BITS + k for k in range(lrows)]
    src_c = pos_w[axis_order[jnp.array(out_local, dtype=jnp.int32)]]
    plan_c = plan_permute(src_c, lrows, lcols)
    return plan_a, plan_c


def regroup(block, plans):
    plan_a, plan_c = plans
    planes, nrow, ncol = block.shape
    devices = lax.axis_size("rows") * lax.axis_size("bond")
    block = apply_permute(block, plan_a)
    block = block.reshape(planes, devices, -1)
    block = lax.all_to_all(block, ("bond", "rows"), split_axis=1, concat_axis=1, tiled=True)
    block = block.reshape(planes, nrow, ncol)
    return apply_permute(block, plan_c)


def per_device(amps_left, amps_right, axis_order):
    plans = make_plans(axis_order)
    gathered = lax.all_gather(amps_right, "rows", axis=1, tiled=True)
    gathered, plans = lax.optimization_barrier((gathered, plans))
    real_part = cross_dot(amps_left[0], gathered[0]) - cross_dot(amps_left[1], gathered[1])
    imag_part = cross_dot(amps_left[0], gathered[1]) + cross_dot(amps_left[1], gathered[0])
    partial_sums = jnp.stack([real_part, imag_part])
    block = lax.psum_scatter(partial_sums, "bond", scatter_dimension=2, tiled=True)
    return regroup(block, plans)


def solution(mesh):
    placed = (P(None, "rows", "bond"), P(None, "rows", "bond"), P())
    return jax.shard_map(
        per_device, mesh=mesh, in_specs=placed, out_specs=P(None, "rows", "bond"), check_vma=False
    )
```

```python
import jax
import jax.numpy as jnp
from jax import lax
from jax.sharding import PartitionSpec as P

ROW_BITS = 12
COL_BITS = 9


def cross_dot(left, right):
    return lax.dot_general(
        left,
        right,
        (((1,), (1,)), ((), ())),
        precision=lax.Precision.HIGH,
        preferred_element_type=jnp.float32,
    )


def rank_within(keys, member):
    below = (keys[None, :] < keys[:, None]) & member[None, :]
    return jnp.sum(below.astype(jnp.int32), axis=1)


def perm_matrix(new_pos, nbits):
    old = jnp.arange(2**nbits, dtype=jnp.int32)
    moved = jnp.zeros_like(old)
    for bit_num in range(nbits):
        moved = moved + jnp.left_shift(jnp.right_shift(old, bit_num) & 1, new_pos[bit_num])
    return (old[:, None] == moved[None, :]).astype(jnp.float32)


def permute_rows(block, mat):
    return jnp.einsum("no,pol->pnl", mat, block, precision=lax.Precision.HIGHEST)


def permute_lanes(block, mat):
    return jnp.einsum("no,pro->prn", mat, block, precision=lax.Precision.HIGHEST)


def cross_swap(block, m, rbits, cbits):
    def branch(k):
        def run(x):
            planes = x.shape[0]
            x = x.reshape(planes, 2 ** (rbits - k), 2**k, 2**k, 2 ** (cbits - k))
            x = jnp.transpose(x, (0, 1, 3, 2, 4))
            return x.reshape(planes, 2**rbits, 2**cbits)

        return run

    return lax.switch(m, [branch(k) for k in range(min(rbits, cbits) + 1)], block)


def plan_permute(src, rbits, cbits):
    total = rbits + cbits
    dest_of = jnp.zeros((total,), jnp.int32).at[src].set(jnp.arange(total, dtype=jnp.int32))
    pos = jnp.arange(total, dtype=jnp.int32)
    is_lane = pos < cbits
    goes_lane = dest_of < cbits
    lane_stay = is_lane & goes_lane
    lane_go = is_lane & ~goes_lane
    row_stay = ~is_lane & ~goes_lane
    row_go = ~is_lane & goes_lane
    m = jnp.sum(row_go.astype(jnp.int32))
    r_lane_stay = rank_within(dest_of, lane_stay)
    r_lane_go = rank_within(dest_of, lane_go)
    r_row_stay = rank_within(dest_of, row_stay)
    r_row_go = rank_within(dest_of, row_go)
    first_rows = jnp.where(row_go, r_row_go, m + r_row_stay)[cbits:]
    first_lanes = jnp.where(lane_go, cbits - m + r_lane_go, r_lane_stay)[:cbits]
    lane_src_pos = jnp.where(lane_stay, r_lane_stay, cbits - m + r_row_go)
    lane_members = lane_stay | row_go
    row_src_pos = jnp.where(lane_go, r_lane_go, m + r_row_stay)
    row_members = lane_go | row_stay
    second_lanes = jnp.zeros((cbits,), jnp.int32).at[
        jnp.where(lane_members, lane_src_pos, cbits)
    ].set(dest_of, mode="drop")
    second_rows = jnp.zeros((rbits,), jnp.int32).at[
        jnp.where(row_members, row_src_pos, rbits)
    ].set(dest_of - cbits, mode="drop")
    mats = (
        perm_matrix(first_rows, rbits),
        perm_matrix(first_lanes, cbits),
        perm_matrix(second_rows, rbits),
        perm_matrix(second_lanes, cbits),
    )
    return mats, m


def apply_permute(block, plan):
    (rows_a, lanes_a, rows_b, lanes_b), m = plan
    rbits = block.shape[1].bit_length() - 1
    cbits = block.shape[2].bit_length() - 1
    block = permute_rows(block, rows_a)
    block = permute_lanes(block, lanes_a)
    block = cross_swap(block, m, rbits, cbits)
    block = permute_rows(block, rows_b)
    return permute_lanes(block, lanes_b)


def make_plans(axis_order):
    nrows = lax.axis_size("rows")
    nbond = lax.axis_size("bond")
    row_devbits = nrows.bit_length() - 1
    bond_devbits = nbond.bit_length() - 1
    total_bits = ROW_BITS + COL_BITS
    lrows = ROW_BITS - row_devbits
    lcols = COL_BITS - bond_devbits
    nlocal = lrows + lcols
    devbits = row_devbits + bond_devbits
    local_of = []
    for bit in range(total_bits):
        if bit < lcols:
            local_of.append(bit)
        elif COL_BITS <= bit < COL_BITS + lrows:
            local_of.append(bit - COL_BITS + lcols)
        else:
            local_of.append(-1)
    local_of = jnp.array(local_of, dtype=jnp.int32)
    out_dev = [COL_BITS + lrows + k for k in range(row_devbits)] + [
        lcols + k for k in range(bond_devbits)
    ]
    dev_src = local_of[axis_order[jnp.array(out_dev, dtype=jnp.int32)]]
    pos = jnp.arange(nlocal, dtype=jnp.int32)
    is_dev = jnp.any(pos[:, None] == dev_src[None, :], axis=1)
    keep = ~is_dev
    keep_rank = rank_within(pos, keep)
    src_a = jnp.zeros((nlocal,), jnp.int32).at[
        jnp.where(keep, keep_rank, nlocal)
    ].set(pos, mode="drop")
    src_a = src_a.at[nlocal - devbits + jnp.arange(devbits)].set(dev_src)
    plan_a = plan_permute(src_a, lrows, lcols)
    src_dev_bits = [COL_BITS + lrows + k for k in range(row_devbits)] + [
        lcols + k for k in range(bond_devbits)
    ]
    pos_w = jnp.full((total_bits,), -1, jnp.int32)
    within = jnp.zeros((nlocal,), jnp.int32).at[jnp.where(keep, keep_rank, nlocal)].set(
        pos, mode="drop"
    )
    prod_of_local = jnp.array(
        [b for b in range(total_bits) if b < lcols]
        + [b for b in range(COL_BITS, COL_BITS + lrows)],
        dtype=jnp.int32,
    )
    pos_w = pos_w.at[prod_of_local[within[: nlocal - devbits]]].set(
        jnp.arange(nlocal - devbits, dtype=jnp.int32)
    )
    pos_w = pos_w.at[jnp.array(src_dev_bits, dtype=jnp.int32)].set(
        nlocal - devbits + jnp.arange(devbits, dtype=jnp.int32)
    )
    out_local = [b for b in range(lcols)] + [COL_BITS + k for k in range(lrows)]
    src_c = pos_w[axis_order[jnp.array(out_local, dtype=jnp.int32)]]
    plan_c = plan_permute(src_c, lrows, lcols)
    return plan_a, plan_c


def regroup(block, plans):
    plan_a, plan_c = plans
    planes, nrow, ncol = block.shape
    devices = lax.axis_size("rows") * lax.axis_size("bond")
    block = apply_permute(block, plan_a)
    block = block.reshape(planes, devices, -1)
    block = lax.all_to_all(block, ("bond", "rows"), split_axis=1, concat_axis=1, tiled=True)
    block = block.reshape(planes, nrow, ncol)
    return apply_permute(block, plan_c)


def ring_all_gather(shard, axis):
    size = lax.axis_size(axis)
    ring = [2 * k for k in range(size // 2)] + [2 * k + 1 for k in reversed(range(size // 2))]
    pos_of = [ring.index(idx) for idx in range(size)]
    fwd = [(ring[i], ring[(i + 1) % size]) for i in range(size)]
    bwd = [(ring[(i + 1) % size], ring[i]) for i in range(size)]
    me = lax.axis_index(axis)
    my_pos = jnp.array(pos_of, dtype=jnp.int32)[me]
    ring_arr = jnp.array(ring, dtype=jnp.int32)
    planes, rows, width = shard.shape
    half = rows // 2
    ahead, behind = shard[:, :half], shard[:, half:]
    zero = jnp.int32(0)
    out = jnp.zeros((planes, size * rows, width), shard.dtype)
    out = lax.dynamic_update_slice(out, shard, (zero, me * rows, zero))
    for step in range(1, size):
        ahead = lax.ppermute(ahead, axis, fwd)
        behind = lax.ppermute(behind, axis, bwd)
        src_ahead = ring_arr[(my_pos - step) % size]
        src_behind = ring_arr[(my_pos + step) % size]
        out = lax.dynamic_update_slice(out, ahead, (zero, src_ahead * rows, zero))
        out = lax.dynamic_update_slice(out, behind, (zero, src_behind * rows + half, zero))
    return out


def per_device(amps_left, amps_right, axis_order):
    plans = make_plans(axis_order)
    gathered = ring_all_gather(amps_right, "rows")
    gathered, plans = lax.optimization_barrier((gathered, plans))
    real_part = cross_dot(amps_left[0], gathered[0]) - cross_dot(amps_left[1], gathered[1])
    imag_part = cross_dot(amps_left[0], gathered[1]) + cross_dot(amps_left[1], gathered[0])
    partial_sums = jnp.stack([real_part, imag_part])
    block = lax.psum_scatter(partial_sums, "bond", scatter_dimension=2, tiled=True)
    return regroup(block, plans)


def solution(mesh):
    placed = (P(None, "rows", "bond"), P(None, "rows", "bond"), P())
    return jax.shard_map(
        per_device, mesh=mesh, in_specs=placed, out_specs=P(None, "rows", "bond"), check_vma=False
    )
```

```python
import jax
import jax.numpy as jnp
from jax import lax
from jax.sharding import PartitionSpec as P

ROW_BITS = 12
COL_BITS = 9


def cross_dot(left, right):
    return lax.dot_general(
        left,
        right,
        (((1,), (1,)), ((), ())),
        precision=lax.Precision.HIGH,
        preferred_element_type=jnp.float32,
    )


def rank_within(keys, member):
    below = (keys[None, :] < keys[:, None]) & member[None, :]
    return jnp.sum(below.astype(jnp.int32), axis=1)


def perm_matrix(new_pos, nbits):
    old = jnp.arange(2**nbits, dtype=jnp.int32)
    moved = jnp.zeros_like(old)
    for bit_num in range(nbits):
        moved = moved + jnp.left_shift(jnp.right_shift(old, bit_num) & 1, new_pos[bit_num])
    moved = lax.optimization_barrier(moved)
    return (old[:, None] == moved[None, :]).astype(jnp.float32)


def permute_rows(block, mat):
    return jnp.einsum("no,pol->pnl", mat, block, precision=lax.Precision.HIGHEST)


def permute_lanes(block, mat):
    return jnp.einsum("no,pro->prn", mat, block, precision=lax.Precision.HIGHEST)


def cross_swap(block, m, rbits, cbits):
    def branch(k):
        def run(x):
            planes = x.shape[0]
            x = x.reshape(planes, 2 ** (rbits - k), 2**k, 2**k, 2 ** (cbits - k))
            x = jnp.transpose(x, (0, 1, 3, 2, 4))
            return x.reshape(planes, 2**rbits, 2**cbits)

        return run

    return lax.switch(m, [branch(k) for k in range(min(rbits, cbits) + 1)], block)


def plan_permute(src, rbits, cbits):
    total = rbits + cbits
    dest_of = jnp.zeros((total,), jnp.int32).at[src].set(jnp.arange(total, dtype=jnp.int32))
    pos = jnp.arange(total, dtype=jnp.int32)
    is_lane = pos < cbits
    goes_lane = dest_of < cbits
    lane_stay = is_lane & goes_lane
    lane_go = is_lane & ~goes_lane
    row_stay = ~is_lane & ~goes_lane
    row_go = ~is_lane & goes_lane
    m = jnp.sum(row_go.astype(jnp.int32))
    r_lane_stay = rank_within(dest_of, lane_stay)
    r_lane_go = rank_within(dest_of, lane_go)
    r_row_stay = rank_within(dest_of, row_stay)
    r_row_go = rank_within(dest_of, row_go)
    first_rows = jnp.where(row_go, r_row_go, m + r_row_stay)[cbits:]
    first_lanes = jnp.where(lane_go, cbits - m + r_lane_go, r_lane_stay)[:cbits]
    lane_src_pos = jnp.where(lane_stay, r_lane_stay, cbits - m + r_row_go)
    lane_members = lane_stay | row_go
    row_src_pos = jnp.where(lane_go, r_lane_go, m + r_row_stay)
    row_members = lane_go | row_stay
    second_lanes = jnp.zeros((cbits,), jnp.int32).at[
        jnp.where(lane_members, lane_src_pos, cbits)
    ].set(dest_of, mode="drop")
    second_rows = jnp.zeros((rbits,), jnp.int32).at[
        jnp.where(row_members, row_src_pos, rbits)
    ].set(dest_of - cbits, mode="drop")
    mats = (
        perm_matrix(first_rows, rbits),
        perm_matrix(first_lanes, cbits),
        perm_matrix(second_rows, rbits),
        perm_matrix(second_lanes, cbits),
    )
    return mats, m


def apply_permute(block, plan):
    (rows_a, lanes_a, rows_b, lanes_b), m = plan
    rbits = block.shape[1].bit_length() - 1
    cbits = block.shape[2].bit_length() - 1
    block = permute_rows(block, rows_a)
    block = permute_lanes(block, lanes_a)
    block = cross_swap(block, m, rbits, cbits)
    block = permute_rows(block, rows_b)
    return permute_lanes(block, lanes_b)


def make_plans(axis_order):
    nrows = lax.axis_size("rows")
    nbond = lax.axis_size("bond")
    row_devbits = nrows.bit_length() - 1
    bond_devbits = nbond.bit_length() - 1
    total_bits = ROW_BITS + COL_BITS
    lrows = ROW_BITS - row_devbits
    lcols = COL_BITS - bond_devbits
    nlocal = lrows + lcols
    devbits = row_devbits + bond_devbits
    local_of = []
    for bit in range(total_bits):
        if bit < lcols:
            local_of.append(bit)
        elif COL_BITS <= bit < COL_BITS + lrows:
            local_of.append(bit - COL_BITS + lcols)
        else:
            local_of.append(-1)
    local_of = jnp.array(local_of, dtype=jnp.int32)
    out_dev = [COL_BITS + lrows + k for k in range(row_devbits)] + [
        lcols + k for k in range(bond_devbits)
    ]
    dev_src = local_of[axis_order[jnp.array(out_dev, dtype=jnp.int32)]]
    pos = jnp.arange(nlocal, dtype=jnp.int32)
    is_dev = jnp.any(pos[:, None] == dev_src[None, :], axis=1)
    keep = ~is_dev
    keep_rank = rank_within(pos, keep)
    src_a = jnp.zeros((nlocal,), jnp.int32).at[
        jnp.where(keep, keep_rank, nlocal)
    ].set(pos, mode="drop")
    src_a = src_a.at[nlocal - devbits + jnp.arange(devbits)].set(dev_src)
    plan_a = plan_permute(src_a, lrows, lcols)
    src_dev_bits = [COL_BITS + lrows + k for k in range(row_devbits)] + [
        lcols + k for k in range(bond_devbits)
    ]
    pos_w = jnp.full((total_bits,), -1, jnp.int32)
    within = jnp.zeros((nlocal,), jnp.int32).at[jnp.where(keep, keep_rank, nlocal)].set(
        pos, mode="drop"
    )
    prod_of_local = jnp.array(
        [b for b in range(total_bits) if b < lcols]
        + [b for b in range(COL_BITS, COL_BITS + lrows)],
        dtype=jnp.int32,
    )
    pos_w = pos_w.at[prod_of_local[within[: nlocal - devbits]]].set(
        jnp.arange(nlocal - devbits, dtype=jnp.int32)
    )
    pos_w = pos_w.at[jnp.array(src_dev_bits, dtype=jnp.int32)].set(
        nlocal - devbits + jnp.arange(devbits, dtype=jnp.int32)
    )
    out_local = [b for b in range(lcols)] + [COL_BITS + k for k in range(lrows)]
    src_c = pos_w[axis_order[jnp.array(out_local, dtype=jnp.int32)]]
    plan_c = plan_permute(src_c, lrows, lcols)
    return plan_a, plan_c


def regroup(block, plans):
    plan_a, plan_c = plans
    planes, nrow, ncol = block.shape
    devices = lax.axis_size("rows") * lax.axis_size("bond")
    block = apply_permute(block, plan_a)
    block = block.reshape(planes, devices, -1)
    block = lax.all_to_all(block, ("bond", "rows"), split_axis=1, concat_axis=1, tiled=True)
    block = block.reshape(planes, nrow, ncol)
    return apply_permute(block, plan_c)


def ring_all_gather(shard, axis):
    size = lax.axis_size(axis)
    ring = [2 * k for k in range(size // 2)] + [2 * k + 1 for k in reversed(range(size // 2))]
    pos_of = [ring.index(idx) for idx in range(size)]
    fwd = [(ring[i], ring[(i + 1) % size]) for i in range(size)]
    bwd = [(ring[(i + 1) % size], ring[i]) for i in range(size)]
    me = lax.axis_index(axis)
    my_pos = jnp.array(pos_of, dtype=jnp.int32)[me]
    ring_arr = jnp.array(ring, dtype=jnp.int32)
    planes, rows, width = shard.shape
    half = rows // 2
    ahead, behind = shard[:, :half], shard[:, half:]
    zero = jnp.int32(0)
    out = jnp.zeros((planes, size * rows, width), shard.dtype)
    out = lax.dynamic_update_slice(out, shard, (zero, me * rows, zero))
    for step in range(1, size):
        ahead = lax.ppermute(ahead, axis, fwd)
        behind = lax.ppermute(behind, axis, bwd)
        src_ahead = ring_arr[(my_pos - step) % size]
        src_behind = ring_arr[(my_pos + step) % size]
        out = lax.dynamic_update_slice(out, ahead, (zero, src_ahead * rows, zero))
        out = lax.dynamic_update_slice(out, behind, (zero, src_behind * rows + half, zero))
    return out


def per_device(amps_left, amps_right, axis_order):
    plans = make_plans(axis_order)
    gathered = ring_all_gather(amps_right, "rows")
    gathered, plans = lax.optimization_barrier((gathered, plans))
    real_part = cross_dot(amps_left[0], gathered[0]) - cross_dot(amps_left[1], gathered[1])
    imag_part = cross_dot(amps_left[0], gathered[1]) + cross_dot(amps_left[1], gathered[0])
    partial_sums = jnp.stack([real_part, imag_part])
    block = lax.psum_scatter(partial_sums, "bond", scatter_dimension=2, tiled=True)
    return regroup(block, plans)


def solution(mesh):
    placed = (P(None, "rows", "bond"), P(None, "rows", "bond"), P())
    return jax.shard_map(
        per_device, mesh=mesh, in_specs=placed, out_specs=P(None, "rows", "bond"), check_vma=False
    )
```

```python
import jax
import jax.numpy as jnp
from jax import lax
from jax.sharding import PartitionSpec as P

ROW_BITS = 12
COL_BITS = 9


def cross_dot(left, right):
    return lax.dot_general(
        left,
        right,
        (((1,), (1,)), ((), ())),
        precision=lax.Precision.HIGH,
        preferred_element_type=jnp.float32,
    )


def rank_within(keys, member):
    below = (keys[None, :] < keys[:, None]) & member[None, :]
    return jnp.sum(below.astype(jnp.int32), axis=1)


def perm_matrix(new_pos, nbits):
    old = jnp.arange(2**nbits, dtype=jnp.int32)
    bits = jnp.right_shift(old[:, None], jnp.arange(nbits, dtype=jnp.int32)[None, :]) & 1
    weights = jnp.left_shift(jnp.int32(1), new_pos)
    moved = jnp.sum(bits * weights[None, :], axis=1)
    moved = lax.optimization_barrier(moved)
    return (old[:, None] == moved[None, :]).astype(jnp.float32)


def permute_rows(block, mat):
    return jnp.einsum("no,pol->pnl", mat, block, precision=lax.Precision.HIGHEST)


def permute_lanes(block, mat):
    return jnp.einsum("no,pro->prn", mat, block, precision=lax.Precision.HIGHEST)


def cross_swap(block, m, rbits, cbits):
    def branch(k):
        def run(x):
            planes = x.shape[0]
            x = x.reshape(planes, 2 ** (rbits - k), 2**k, 2**k, 2 ** (cbits - k))
            x = jnp.transpose(x, (0, 1, 3, 2, 4))
            return x.reshape(planes, 2**rbits, 2**cbits)

        return run

    return lax.switch(m, [branch(k) for k in range(min(rbits, cbits) + 1)], block)


def plan_permute(src, rbits, cbits):
    total = rbits + cbits
    dest_of = jnp.zeros((total,), jnp.int32).at[src].set(jnp.arange(total, dtype=jnp.int32))
    pos = jnp.arange(total, dtype=jnp.int32)
    is_lane = pos < cbits
    goes_lane = dest_of < cbits
    lane_stay = is_lane & goes_lane
    lane_go = is_lane & ~goes_lane
    row_stay = ~is_lane & ~goes_lane
    row_go = ~is_lane & goes_lane
    m = jnp.sum(row_go.astype(jnp.int32))
    r_lane_stay = rank_within(dest_of, lane_stay)
    r_lane_go = rank_within(dest_of, lane_go)
    r_row_stay = rank_within(dest_of, row_stay)
    r_row_go = rank_within(dest_of, row_go)
    first_rows = jnp.where(row_go, r_row_go, m + r_row_stay)[cbits:]
    first_lanes = jnp.where(lane_go, cbits - m + r_lane_go, r_lane_stay)[:cbits]
    lane_src_pos = jnp.where(lane_stay, r_lane_stay, cbits - m + r_row_go)
    lane_members = lane_stay | row_go
    row_src_pos = jnp.where(lane_go, r_lane_go, m + r_row_stay)
    row_members = lane_go | row_stay
    second_lanes = jnp.zeros((cbits,), jnp.int32).at[
        jnp.where(lane_members, lane_src_pos, cbits)
    ].set(dest_of, mode="drop")
    second_rows = jnp.zeros((rbits,), jnp.int32).at[
        jnp.where(row_members, row_src_pos, rbits)
    ].set(dest_of - cbits, mode="drop")
    mats = (
        perm_matrix(first_rows, rbits),
        perm_matrix(first_lanes, cbits),
        perm_matrix(second_rows, rbits),
        perm_matrix(second_lanes, cbits),
    )
    return mats, m


def apply_permute(block, plan):
    (rows_a, lanes_a, rows_b, lanes_b), m = plan
    rbits = block.shape[1].bit_length() - 1
    cbits = block.shape[2].bit_length() - 1
    block = permute_rows(block, rows_a)
    block = permute_lanes(block, lanes_a)
    block = cross_swap(block, m, rbits, cbits)
    block = permute_rows(block, rows_b)
    return permute_lanes(block, lanes_b)


def make_plans(axis_order):
    nrows = lax.axis_size("rows")
    nbond = lax.axis_size("bond")
    row_devbits = nrows.bit_length() - 1
    bond_devbits = nbond.bit_length() - 1
    total_bits = ROW_BITS + COL_BITS
    lrows = ROW_BITS - row_devbits
    lcols = COL_BITS - bond_devbits
    nlocal = lrows + lcols
    devbits = row_devbits + bond_devbits
    local_of = []
    for bit in range(total_bits):
        if bit < lcols:
            local_of.append(bit)
        elif COL_BITS <= bit < COL_BITS + lrows:
            local_of.append(bit - COL_BITS + lcols)
        else:
            local_of.append(-1)
    local_of = jnp.array(local_of, dtype=jnp.int32)
    out_dev = [COL_BITS + lrows + k for k in range(row_devbits)] + [
        lcols + k for k in range(bond_devbits)
    ]
    dev_src = local_of[axis_order[jnp.array(out_dev, dtype=jnp.int32)]]
    pos = jnp.arange(nlocal, dtype=jnp.int32)
    is_dev = jnp.any(pos[:, None] == dev_src[None, :], axis=1)
    keep = ~is_dev
    keep_rank = rank_within(pos, keep)
    src_a = jnp.zeros((nlocal,), jnp.int32).at[
        jnp.where(keep, keep_rank, nlocal)
    ].set(pos, mode="drop")
    src_a = src_a.at[nlocal - devbits + jnp.arange(devbits)].set(dev_src)
    plan_a = plan_permute(src_a, lrows, lcols)
    src_dev_bits = [COL_BITS + lrows + k for k in range(row_devbits)] + [
        lcols + k for k in range(bond_devbits)
    ]
    pos_w = jnp.full((total_bits,), -1, jnp.int32)
    within = jnp.zeros((nlocal,), jnp.int32).at[jnp.where(keep, keep_rank, nlocal)].set(
        pos, mode="drop"
    )
    prod_of_local = jnp.array(
        [b for b in range(total_bits) if b < lcols]
        + [b for b in range(COL_BITS, COL_BITS + lrows)],
        dtype=jnp.int32,
    )
    pos_w = pos_w.at[prod_of_local[within[: nlocal - devbits]]].set(
        jnp.arange(nlocal - devbits, dtype=jnp.int32)
    )
    pos_w = pos_w.at[jnp.array(src_dev_bits, dtype=jnp.int32)].set(
        nlocal - devbits + jnp.arange(devbits, dtype=jnp.int32)
    )
    out_local = [b for b in range(lcols)] + [COL_BITS + k for k in range(lrows)]
    src_c = pos_w[axis_order[jnp.array(out_local, dtype=jnp.int32)]]
    plan_c = plan_permute(src_c, lrows, lcols)
    return plan_a, plan_c


def regroup(block, plans):
    plan_a, plan_c = plans
    planes, nrow, ncol = block.shape
    devices = lax.axis_size("rows") * lax.axis_size("bond")
    block = apply_permute(block, plan_a)
    block = block.reshape(planes, devices, -1)
    block = lax.all_to_all(block, ("bond", "rows"), split_axis=1, concat_axis=1, tiled=True)
    block = block.reshape(planes, nrow, ncol)
    return apply_permute(block, plan_c)


def ring_all_gather(shard, axis):
    size = lax.axis_size(axis)
    ring = [2 * k for k in range(size // 2)] + [2 * k + 1 for k in reversed(range(size // 2))]
    pos_of = [ring.index(idx) for idx in range(size)]
    fwd = [(ring[i], ring[(i + 1) % size]) for i in range(size)]
    bwd = [(ring[(i + 1) % size], ring[i]) for i in range(size)]
    me = lax.axis_index(axis)
    my_pos = jnp.array(pos_of, dtype=jnp.int32)[me]
    ring_arr = jnp.array(ring, dtype=jnp.int32)
    planes, rows, width = shard.shape
    half = rows // 2
    ahead, behind = shard[:, :half], shard[:, half:]
    zero = jnp.int32(0)
    out = jnp.zeros((planes, size * rows, width), shard.dtype)
    out = lax.dynamic_update_slice(out, shard, (zero, me * rows, zero))
    for step in range(1, size):
        ahead = lax.ppermute(ahead, axis, fwd)
        behind = lax.ppermute(behind, axis, bwd)
        src_ahead = ring_arr[(my_pos - step) % size]
        src_behind = ring_arr[(my_pos + step) % size]
        out = lax.dynamic_update_slice(out, ahead, (zero, src_ahead * rows, zero))
        out = lax.dynamic_update_slice(out, behind, (zero, src_behind * rows + half, zero))
    return out


def per_device(amps_left, amps_right, axis_order):
    plans = make_plans(axis_order)
    gathered = ring_all_gather(amps_right, "rows")
    gathered, plans = lax.optimization_barrier((gathered, plans))
    real_part = cross_dot(amps_left[0], gathered[0]) - cross_dot(amps_left[1], gathered[1])
    imag_part = cross_dot(amps_left[0], gathered[1]) + cross_dot(amps_left[1], gathered[0])
    partial_sums = jnp.stack([real_part, imag_part])
    block = lax.psum_scatter(partial_sums, "bond", scatter_dimension=2, tiled=True)
    return regroup(block, plans)


def solution(mesh):
    placed = (P(None, "rows", "bond"), P(None, "rows", "bond"), P())
    return jax.shard_map(
        per_device, mesh=mesh, in_specs=placed, out_specs=P(None, "rows", "bond"), check_vma=False
    )
```

```python
import jax
import jax.numpy as jnp
from jax import lax
from jax.sharding import PartitionSpec as P

ROW_BITS = 12
COL_BITS = 9


def cross_dot(left, right):
    return lax.dot_general(
        left,
        right,
        (((1,), (1,)), ((), ())),
        precision=lax.Precision.HIGH,
        preferred_element_type=jnp.float32,
    )


def rank_within(keys, member):
    below = (keys[None, :] < keys[:, None]) & member[None, :]
    return jnp.sum(below.astype(jnp.int32), axis=1)


def perm_matrix(new_pos, nbits):
    old = jnp.arange(2**nbits, dtype=jnp.int32)
    bits = jnp.right_shift(old[:, None], jnp.arange(nbits, dtype=jnp.int32)[None, :]) & 1
    weights = jnp.left_shift(jnp.int32(1), new_pos)
    moved = jnp.sum(bits * weights[None, :], axis=1)
    moved = lax.optimization_barrier(moved)
    return (old[:, None] == moved[None, :]).astype(jnp.float32)


def permute_rows(block, mat):
    return jnp.einsum("no,pol->pnl", mat, block, precision=lax.Precision.HIGHEST)


def permute_lanes(block, mat):
    return jnp.einsum("no,pro->prn", mat, block, precision=lax.Precision.HIGHEST)


def cross_swap(block, m, rbits, cbits):
    def branch(k):
        def run(x):
            planes = x.shape[0]
            x = x.reshape(planes, 2 ** (rbits - k), 2**k, 2**k, 2 ** (cbits - k))
            x = jnp.transpose(x, (0, 1, 3, 2, 4))
            return x.reshape(planes, 2**rbits, 2**cbits)

        return run

    return lax.switch(m, [branch(k) for k in range(min(rbits, cbits) + 1)], block)


def plan_permute(src, rbits, cbits):
    total = rbits + cbits
    dest_of = jnp.zeros((total,), jnp.int32).at[src].set(jnp.arange(total, dtype=jnp.int32))
    pos = jnp.arange(total, dtype=jnp.int32)
    is_lane = pos < cbits
    goes_lane = dest_of < cbits
    lane_stay = is_lane & goes_lane
    lane_go = is_lane & ~goes_lane
    row_stay = ~is_lane & ~goes_lane
    row_go = ~is_lane & goes_lane
    m = jnp.sum(row_go.astype(jnp.int32))
    r_lane_stay = rank_within(dest_of, lane_stay)
    r_lane_go = rank_within(dest_of, lane_go)
    r_row_stay = rank_within(dest_of, row_stay)
    r_row_go = rank_within(dest_of, row_go)
    first_rows = jnp.where(row_go, r_row_go, m + r_row_stay)[cbits:]
    first_lanes = jnp.where(lane_go, cbits - m + r_lane_go, r_lane_stay)[:cbits]
    lane_src_pos = jnp.where(lane_stay, r_lane_stay, cbits - m + r_row_go)
    lane_members = lane_stay | row_go
    row_src_pos = jnp.where(lane_go, r_lane_go, m + r_row_stay)
    row_members = lane_go | row_stay
    second_lanes = jnp.zeros((cbits,), jnp.int32).at[
        jnp.where(lane_members, lane_src_pos, cbits)
    ].set(dest_of, mode="drop")
    second_rows = jnp.zeros((rbits,), jnp.int32).at[
        jnp.where(row_members, row_src_pos, rbits)
    ].set(dest_of - cbits, mode="drop")
    mats = (
        perm_matrix(first_rows, rbits),
        perm_matrix(first_lanes, cbits),
        perm_matrix(second_rows, rbits),
        perm_matrix(second_lanes, cbits),
    )
    return mats, m


def apply_permute(block, plan):
    (rows_a, lanes_a, rows_b, lanes_b), m = plan
    rbits = block.shape[1].bit_length() - 1
    cbits = block.shape[2].bit_length() - 1
    block = permute_rows(block, rows_a)
    block = permute_lanes(block, lanes_a)
    block = cross_swap(block, m, rbits, cbits)
    block = permute_rows(block, rows_b)
    return permute_lanes(block, lanes_b)


def make_plans(axis_order):
    nrows = lax.axis_size("rows")
    nbond = lax.axis_size("bond")
    row_devbits = nrows.bit_length() - 1
    bond_devbits = nbond.bit_length() - 1
    total_bits = ROW_BITS + COL_BITS
    lrows = ROW_BITS - row_devbits
    lcols = COL_BITS - bond_devbits
    prows = lrows - bond_devbits
    nlocal = lrows + lcols
    devbits = row_devbits + bond_devbits
    local_of = jnp.array(
        [bit if bit < nlocal else -1 for bit in range(total_bits)], dtype=jnp.int32
    )
    out_dev = [COL_BITS + lrows + k for k in range(row_devbits)] + [
        lcols + k for k in range(bond_devbits)
    ]
    dev_src = local_of[axis_order[jnp.array(out_dev, dtype=jnp.int32)]]
    pos = jnp.arange(nlocal, dtype=jnp.int32)
    is_dev = jnp.any(pos[:, None] == dev_src[None, :], axis=1)
    keep = ~is_dev
    keep_rank = rank_within(pos, keep)
    within = jnp.zeros((nlocal,), jnp.int32).at[jnp.where(keep, keep_rank, nlocal)].set(
        pos, mode="drop"
    )
    src_a = within.at[nlocal - devbits + jnp.arange(devbits)].set(dev_src)
    plan_a = plan_permute(src_a, prows, COL_BITS)
    src_dev_bits = [COL_BITS + lrows + k for k in range(row_devbits)] + [
        COL_BITS + prows + k for k in range(bond_devbits)
    ]
    pos_w = jnp.full((total_bits,), -1, jnp.int32)
    pos_w = pos_w.at[within[: nlocal - devbits]].set(jnp.arange(nlocal - devbits, dtype=jnp.int32))
    pos_w = pos_w.at[jnp.array(src_dev_bits, dtype=jnp.int32)].set(
        nlocal - devbits + jnp.arange(devbits, dtype=jnp.int32)
    )
    out_local = [b for b in range(lcols)] + [COL_BITS + k for k in range(lrows)]
    src_c = pos_w[axis_order[jnp.array(out_local, dtype=jnp.int32)]]
    plan_c = plan_permute(src_c, lrows, lcols)
    return plan_a, plan_c


def regroup(block, plans):
    plan_a, plan_c = plans
    planes = block.shape[0]
    nrows = lax.axis_size("rows")
    nbond = lax.axis_size("bond")
    lrows = 2**ROW_BITS // nrows
    lcols = 2**COL_BITS // nbond
    block = apply_permute(block, plan_a)
    block = block.reshape(planes, nrows * nbond, -1)
    block = lax.all_to_all(block, ("bond", "rows"), split_axis=1, concat_axis=1, tiled=True)
    block = block.reshape(planes, lrows, lcols)
    return apply_permute(block, plan_c)


def ring_all_gather(shard, axis):
    size = lax.axis_size(axis)
    ring = [2 * k for k in range(size // 2)] + [2 * k + 1 for k in reversed(range(size // 2))]
    pos_of = [ring.index(idx) for idx in range(size)]
    fwd = [(ring[i], ring[(i + 1) % size]) for i in range(size)]
    bwd = [(ring[(i + 1) % size], ring[i]) for i in range(size)]
    me = lax.axis_index(axis)
    my_pos = jnp.array(pos_of, dtype=jnp.int32)[me]
    ring_arr = jnp.array(ring, dtype=jnp.int32)
    planes, rows, width = shard.shape
    half = rows // 2
    ahead, behind = shard[:, :half], shard[:, half:]
    zero = jnp.int32(0)
    out = jnp.zeros((planes, size * rows, width), shard.dtype)
    out = lax.dynamic_update_slice(out, shard, (zero, me * rows, zero))
    for step in range(1, size):
        ahead = lax.ppermute(ahead, axis, fwd)
        behind = lax.ppermute(behind, axis, bwd)
        src_ahead = ring_arr[(my_pos - step) % size]
        src_behind = ring_arr[(my_pos + step) % size]
        out = lax.dynamic_update_slice(out, ahead, (zero, src_ahead * rows, zero))
        out = lax.dynamic_update_slice(out, behind, (zero, src_behind * rows + half, zero))
    return out


def per_device(amps_left, amps_right, axis_order):
    plans = make_plans(axis_order)
    gathered = ring_all_gather(amps_right, "rows")
    gathered, plans = lax.optimization_barrier((gathered, plans))
    real_part = cross_dot(amps_left[0], gathered[0]) - cross_dot(amps_left[1], gathered[1])
    imag_part = cross_dot(amps_left[0], gathered[1]) + cross_dot(amps_left[1], gathered[0])
    partial_sums = jnp.stack([real_part, imag_part])
    block = lax.psum_scatter(partial_sums, "bond", scatter_dimension=1, tiled=True)
    return regroup(block, plans)


def solution(mesh):
    placed = (P(None, "rows", "bond"), P(None, "rows", "bond"), P())
    return jax.shard_map(
        per_device, mesh=mesh, in_specs=placed, out_specs=P(None, "rows", "bond"), check_vma=False
    )
```

```python
import jax
import jax.numpy as jnp
from jax import lax
from jax.sharding import PartitionSpec as P

ROW_BITS = 12
COL_BITS = 9


def cross_dot(left, right):
    return lax.dot_general(
        left,
        right,
        (((1,), (1,)), ((), ())),
        precision=lax.Precision.HIGH,
        preferred_element_type=jnp.float32,
    )


def rank_within(keys, member):
    below = (keys[None, :] < keys[:, None]) & member[None, :]
    return jnp.sum(below.astype(jnp.int32), axis=1)


def perm_matrix(new_pos, nbits):
    old = jnp.arange(2**nbits, dtype=jnp.int32)
    bits = jnp.right_shift(old[:, None], jnp.arange(nbits, dtype=jnp.int32)[None, :]) & 1
    weights = jnp.left_shift(jnp.int32(1), new_pos)
    moved = jnp.sum(bits * weights[None, :], axis=1)
    moved = lax.optimization_barrier(moved)
    return (old[:, None] == moved[None, :]).astype(jnp.float32)


def permute_rows(block, mat):
    return jnp.einsum("no,pol->pnl", mat, block, precision=lax.Precision.HIGH)


def permute_lanes(block, mat):
    return jnp.einsum("no,pro->prn", mat, block, precision=lax.Precision.HIGH)


def cross_swap(block, m, rbits, cbits):
    def branch(k):
        def run(x):
            planes = x.shape[0]
            x = x.reshape(planes, 2 ** (rbits - k), 2**k, 2**k, 2 ** (cbits - k))
            x = jnp.transpose(x, (0, 1, 3, 2, 4))
            return x.reshape(planes, 2**rbits, 2**cbits)

        return run

    return lax.switch(m, [branch(k) for k in range(min(rbits, cbits) + 1)], block)


def plan_permute(src, rbits, cbits):
    total = rbits + cbits
    dest_of = jnp.zeros((total,), jnp.int32).at[src].set(jnp.arange(total, dtype=jnp.int32))
    pos = jnp.arange(total, dtype=jnp.int32)
    is_lane = pos < cbits
    goes_lane = dest_of < cbits
    lane_stay = is_lane & goes_lane
    lane_go = is_lane & ~goes_lane
    row_stay = ~is_lane & ~goes_lane
    row_go = ~is_lane & goes_lane
    m = jnp.sum(row_go.astype(jnp.int32))
    r_lane_stay = rank_within(dest_of, lane_stay)
    r_lane_go = rank_within(dest_of, lane_go)
    r_row_stay = rank_within(dest_of, row_stay)
    r_row_go = rank_within(dest_of, row_go)
    first_rows = jnp.where(row_go, r_row_go, m + r_row_stay)[cbits:]
    first_lanes = jnp.where(lane_go, cbits - m + r_lane_go, r_lane_stay)[:cbits]
    lane_src_pos = jnp.where(lane_stay, r_lane_stay, cbits - m + r_row_go)
    lane_members = lane_stay | row_go
    row_src_pos = jnp.where(lane_go, r_lane_go, m + r_row_stay)
    row_members = lane_go | row_stay
    second_lanes = jnp.zeros((cbits,), jnp.int32).at[
        jnp.where(lane_members, lane_src_pos, cbits)
    ].set(dest_of, mode="drop")
    second_rows = jnp.zeros((rbits,), jnp.int32).at[
        jnp.where(row_members, row_src_pos, rbits)
    ].set(dest_of - cbits, mode="drop")
    mats = (
        perm_matrix(first_rows, rbits),
        perm_matrix(first_lanes, cbits),
        perm_matrix(second_rows, rbits),
        perm_matrix(second_lanes, cbits),
    )
    return mats, m


def apply_permute(block, plan):
    (rows_a, lanes_a, rows_b, lanes_b), m = plan
    rbits = block.shape[1].bit_length() - 1
    cbits = block.shape[2].bit_length() - 1
    block = permute_rows(block, rows_a)
    block = permute_lanes(block, lanes_a)
    block = cross_swap(block, m, rbits, cbits)
    block = permute_rows(block, rows_b)
    return permute_lanes(block, lanes_b)


def make_plans(axis_order):
    nrows = lax.axis_size("rows")
    nbond = lax.axis_size("bond")
    row_devbits = nrows.bit_length() - 1
    bond_devbits = nbond.bit_length() - 1
    total_bits = ROW_BITS + COL_BITS
    lrows = ROW_BITS - row_devbits
    lcols = COL_BITS - bond_devbits
    prows = lrows - bond_devbits
    nlocal = lrows + lcols
    devbits = row_devbits + bond_devbits
    local_of = jnp.array(
        [bit if bit < nlocal else -1 for bit in range(total_bits)], dtype=jnp.int32
    )
    out_dev = [COL_BITS + lrows + k for k in range(row_devbits)] + [
        lcols + k for k in range(bond_devbits)
    ]
    dev_src = local_of[axis_order[jnp.array(out_dev, dtype=jnp.int32)]]
    pos = jnp.arange(nlocal, dtype=jnp.int32)
    is_dev = jnp.any(pos[:, None] == dev_src[None, :], axis=1)
    keep = ~is_dev
    keep_rank = rank_within(pos, keep)
    within = jnp.zeros((nlocal,), jnp.int32).at[jnp.where(keep, keep_rank, nlocal)].set(
        pos, mode="drop"
    )
    src_a = within.at[nlocal - devbits + jnp.arange(devbits)].set(dev_src)
    plan_a = plan_permute(src_a, prows, COL_BITS)
    src_dev_bits = [COL_BITS + lrows + k for k in range(row_devbits)] + [
        COL_BITS + prows + k for k in range(bond_devbits)
    ]
    pos_w = jnp.full((total_bits,), -1, jnp.int32)
    pos_w = pos_w.at[within[: nlocal - devbits]].set(jnp.arange(nlocal - devbits, dtype=jnp.int32))
    pos_w = pos_w.at[jnp.array(src_dev_bits, dtype=jnp.int32)].set(
        nlocal - devbits + jnp.arange(devbits, dtype=jnp.int32)
    )
    out_local = [b for b in range(lcols)] + [COL_BITS + k for k in range(lrows)]
    src_c = pos_w[axis_order[jnp.array(out_local, dtype=jnp.int32)]]
    plan_c = plan_permute(src_c, lrows, lcols)
    return plan_a, plan_c


def regroup(block, plans):
    plan_a, plan_c = plans
    planes = block.shape[0]
    nrows = lax.axis_size("rows")
    nbond = lax.axis_size("bond")
    lrows = 2**ROW_BITS // nrows
    lcols = 2**COL_BITS // nbond
    block = apply_permute(block, plan_a)
    block = block.reshape(planes, nrows * nbond, -1)
    block = lax.all_to_all(block, ("bond", "rows"), split_axis=1, concat_axis=1, tiled=True)
    block = block.reshape(planes, lrows, lcols)
    return apply_permute(block, plan_c)


def ring_all_gather(shard, axis):
    size = lax.axis_size(axis)
    ring = [2 * k for k in range(size // 2)] + [2 * k + 1 for k in reversed(range(size // 2))]
    pos_of = [ring.index(idx) for idx in range(size)]
    fwd = [(ring[i], ring[(i + 1) % size]) for i in range(size)]
    bwd = [(ring[(i + 1) % size], ring[i]) for i in range(size)]
    me = lax.axis_index(axis)
    my_pos = jnp.array(pos_of, dtype=jnp.int32)[me]
    ring_arr = jnp.array(ring, dtype=jnp.int32)
    planes, rows, width = shard.shape
    half = rows // 2
    ahead, behind = shard[:, :half], shard[:, half:]
    zero = jnp.int32(0)
    out = jnp.zeros((planes, size * rows, width), shard.dtype)
    out = lax.dynamic_update_slice(out, shard, (zero, me * rows, zero))
    for step in range(1, size):
        ahead = lax.ppermute(ahead, axis, fwd)
        behind = lax.ppermute(behind, axis, bwd)
        src_ahead = ring_arr[(my_pos - step) % size]
        src_behind = ring_arr[(my_pos + step) % size]
        out = lax.dynamic_update_slice(out, ahead, (zero, src_ahead * rows, zero))
        out = lax.dynamic_update_slice(out, behind, (zero, src_behind * rows + half, zero))
    return out


def per_device(amps_left, amps_right, axis_order):
    plans = make_plans(axis_order)
    gathered = ring_all_gather(amps_right, "rows")
    gathered, plans = lax.optimization_barrier((gathered, plans))
    real_part = cross_dot(amps_left[0], gathered[0]) - cross_dot(amps_left[1], gathered[1])
    imag_part = cross_dot(amps_left[0], gathered[1]) + cross_dot(amps_left[1], gathered[0])
    partial_sums = jnp.stack([real_part, imag_part])
    block = lax.psum_scatter(partial_sums, "bond", scatter_dimension=1, tiled=True)
    return regroup(block, plans)


def solution(mesh):
    placed = (P(None, "rows", "bond"), P(None, "rows", "bond"), P())
    return jax.shard_map(
        per_device, mesh=mesh, in_specs=placed, out_specs=P(None, "rows", "bond"), check_vma=False
    )
```

```python
import jax
import jax.numpy as jnp
from jax import lax
from jax.sharding import PartitionSpec as P

ROW_BITS = 12
COL_BITS = 9


def cross_dot(left, right):
    return lax.dot_general(
        left,
        right,
        (((1,), (1,)), ((), ())),
        precision=lax.Precision.HIGH,
        preferred_element_type=jnp.float32,
    )


def rank_within(keys, member):
    below = (keys[None, :] < keys[:, None]) & member[None, :]
    return jnp.sum(below.astype(jnp.int32), axis=1)


def perm_matrix(new_pos, nbits):
    old = jnp.arange(2**nbits, dtype=jnp.int32)
    bits = jnp.right_shift(old[:, None], jnp.arange(nbits, dtype=jnp.int32)[None, :]) & 1
    weights = jnp.left_shift(jnp.int32(1), new_pos)
    moved = jnp.sum(bits * weights[None, :], axis=1)
    moved = lax.optimization_barrier(moved)
    return (old[:, None] == moved[None, :]).astype(jnp.float32)


def permute_rows(block, mat):
    return jnp.einsum("no,pol->pnl", mat, block, precision=lax.Precision.HIGH)


def permute_lanes(block, mat):
    return jnp.einsum("no,pro->prn", mat, block, precision=lax.Precision.HIGH)


def cross_swap(block, m, rbits, cbits):
    def branch(k):
        def run(x):
            planes = x.shape[0]
            x = x.reshape(planes, 2 ** (rbits - k), 2**k, 2**k, 2 ** (cbits - k))
            x = jnp.transpose(x, (0, 1, 3, 2, 4))
            return x.reshape(planes, 2**rbits, 2**cbits)

        return run

    return lax.switch(m, [branch(k) for k in range(min(rbits, cbits) + 1)], block)


def plan_permute(src, rbits, cbits):
    total = rbits + cbits
    dest_of = jnp.zeros((total,), jnp.int32).at[src].set(jnp.arange(total, dtype=jnp.int32))
    pos = jnp.arange(total, dtype=jnp.int32)
    is_lane = pos < cbits
    goes_lane = dest_of < cbits
    lane_stay = is_lane & goes_lane
    lane_go = is_lane & ~goes_lane
    row_stay = ~is_lane & ~goes_lane
    row_go = ~is_lane & goes_lane
    m = jnp.sum(row_go.astype(jnp.int32))
    r_lane_stay = rank_within(dest_of, lane_stay)
    r_lane_go = rank_within(dest_of, lane_go)
    r_row_stay = rank_within(dest_of, row_stay)
    r_row_go = rank_within(dest_of, row_go)
    first_rows = jnp.where(row_go, r_row_go, m + r_row_stay)[cbits:]
    first_lanes = jnp.where(lane_go, cbits - m + r_lane_go, r_lane_stay)[:cbits]
    lane_src_pos = jnp.where(lane_stay, r_lane_stay, cbits - m + r_row_go)
    lane_members = lane_stay | row_go
    row_src_pos = jnp.where(lane_go, r_lane_go, m + r_row_stay)
    row_members = lane_go | row_stay
    second_lanes = jnp.zeros((cbits,), jnp.int32).at[
        jnp.where(lane_members, lane_src_pos, cbits)
    ].set(dest_of, mode="drop")
    second_rows = jnp.zeros((rbits,), jnp.int32).at[
        jnp.where(row_members, row_src_pos, rbits)
    ].set(dest_of - cbits, mode="drop")
    mats = (
        perm_matrix(first_rows, rbits),
        perm_matrix(first_lanes, cbits),
        perm_matrix(second_rows, rbits),
        perm_matrix(second_lanes, cbits),
    )
    return mats, m


def apply_permute(block, plan):
    (rows_a, lanes_a, rows_b, lanes_b), m = plan
    rbits = block.shape[1].bit_length() - 1
    cbits = block.shape[2].bit_length() - 1
    block = permute_rows(block, rows_a)
    block = permute_lanes(block, lanes_a)
    block = cross_swap(block, m, rbits, cbits)
    block = permute_rows(block, rows_b)
    return permute_lanes(block, lanes_b)


def make_plans(axis_order):
    nrows = lax.axis_size("rows")
    nbond = lax.axis_size("bond")
    row_devbits = nrows.bit_length() - 1
    bond_devbits = nbond.bit_length() - 1
    total_bits = ROW_BITS + COL_BITS
    lrows = ROW_BITS - row_devbits
    lcols = COL_BITS - bond_devbits
    prows = lrows - bond_devbits
    nlocal = lrows + lcols
    devbits = row_devbits + bond_devbits
    local_of = jnp.array(
        [bit if bit < nlocal else -1 for bit in range(total_bits)], dtype=jnp.int32
    )
    out_dev = [COL_BITS + lrows + k for k in range(row_devbits)] + [
        lcols + k for k in range(bond_devbits)
    ]
    dev_src = local_of[axis_order[jnp.array(out_dev, dtype=jnp.int32)]]
    pos = jnp.arange(nlocal, dtype=jnp.int32)
    is_dev = jnp.any(pos[:, None] == dev_src[None, :], axis=1)
    keep = ~is_dev
    keep_rank = rank_within(pos, keep)
    within = jnp.zeros((nlocal,), jnp.int32).at[jnp.where(keep, keep_rank, nlocal)].set(
        pos, mode="drop"
    )
    src_a = within.at[nlocal - devbits + jnp.arange(devbits)].set(dev_src)
    plan_a = plan_permute(src_a, prows, COL_BITS)
    src_dev_bits = [COL_BITS + lrows + k for k in range(row_devbits)] + [
        COL_BITS + prows + k for k in range(bond_devbits)
    ]
    pos_w = jnp.full((total_bits,), -1, jnp.int32)
    pos_w = pos_w.at[within[: nlocal - devbits]].set(jnp.arange(nlocal - devbits, dtype=jnp.int32))
    pos_w = pos_w.at[jnp.array(src_dev_bits, dtype=jnp.int32)].set(
        nlocal - devbits + jnp.arange(devbits, dtype=jnp.int32)
    )
    out_local = [b for b in range(lcols)] + [COL_BITS + k for k in range(lrows)]
    src_c = pos_w[axis_order[jnp.array(out_local, dtype=jnp.int32)]]
    plan_c = plan_permute(src_c, lrows, lcols)
    return plan_a, plan_c


def regroup(block, plans):
    plan_a, plan_c = plans
    planes = block.shape[0]
    nrows = lax.axis_size("rows")
    nbond = lax.axis_size("bond")
    lrows = 2**ROW_BITS // nrows
    lcols = 2**COL_BITS // nbond
    block = apply_permute(block, plan_a)
    block = block.reshape(planes, nrows * nbond, -1)
    block = lax.all_to_all(block, ("bond", "rows"), split_axis=1, concat_axis=1, tiled=True)
    block = block.reshape(planes, lrows, lcols)
    return apply_permute(block, plan_c)


def ring_all_gather(shard, axis):
    size = lax.axis_size(axis)
    ring = [2 * k for k in range(size // 2)] + [2 * k + 1 for k in reversed(range(size // 2))]
    pos_of = [ring.index(idx) for idx in range(size)]
    fwd = [(ring[i], ring[(i + 1) % size]) for i in range(size)]
    bwd = [(ring[(i + 1) % size], ring[i]) for i in range(size)]
    me = lax.axis_index(axis)
    my_pos = jnp.array(pos_of, dtype=jnp.int32)[me]
    ring_arr = jnp.array(ring, dtype=jnp.int32)
    planes, rows, width = shard.shape
    half = rows // 2
    ahead, behind = shard[:, :half], shard[:, half:]
    zero = jnp.int32(0)
    out = jnp.zeros((planes, size * rows, width), shard.dtype)
    out = lax.dynamic_update_slice(out, shard, (zero, me * rows, zero))
    for step in range(1, size):
        ahead = lax.ppermute(ahead, axis, fwd)
        behind = lax.ppermute(behind, axis, bwd)
        src_ahead = ring_arr[(my_pos - step) % size]
        src_behind = ring_arr[(my_pos + step) % size]
        out = lax.dynamic_update_slice(out, ahead, (zero, src_ahead * rows, zero))
        out = lax.dynamic_update_slice(out, behind, (zero, src_behind * rows + half, zero))
    return out


def per_device(amps_left, amps_right, axis_order):
    plans = make_plans(axis_order)
    gathered = ring_all_gather(amps_right, "rows")
    gathered, plans = lax.optimization_barrier((gathered, plans))
    real_part = cross_dot(amps_left[0], gathered[0]) - cross_dot(amps_left[1], gathered[1])
    real_block = lax.psum_scatter(real_part, "bond", scatter_dimension=0, tiled=True)
    imag_part = cross_dot(amps_left[0], gathered[1]) + cross_dot(amps_left[1], gathered[0])
    imag_block = lax.psum_scatter(imag_part, "bond", scatter_dimension=0, tiled=True)
    block = jnp.stack([real_block, imag_block])
    return regroup(block, plans)


def solution(mesh):
    placed = (P(None, "rows", "bond"), P(None, "rows", "bond"), P())
    return jax.shard_map(
        per_device, mesh=mesh, in_specs=placed, out_specs=P(None, "rows", "bond"), check_vma=False
    )
```

```python
import jax
import jax.numpy as jnp
from jax import lax
from jax.sharding import PartitionSpec as P

ROW_BITS = 12
COL_BITS = 9


def cross_dot(left, right):
    return lax.dot_general(
        left,
        right,
        (((1,), (1,)), ((), ())),
        precision=lax.Precision.HIGH,
        preferred_element_type=jnp.float32,
    )


def rank_within(keys, member):
    below = (keys[None, :] < keys[:, None]) & member[None, :]
    return jnp.sum(below.astype(jnp.int32), axis=1)


def perm_matrix(new_pos, nbits):
    old = jnp.arange(2**nbits, dtype=jnp.int32)
    bits = jnp.right_shift(old[:, None], jnp.arange(nbits, dtype=jnp.int32)[None, :]) & 1
    weights = jnp.left_shift(jnp.int32(1), new_pos)
    moved = jnp.sum(bits * weights[None, :], axis=1)
    moved = lax.optimization_barrier(moved)
    return (old[:, None] == moved[None, :]).astype(jnp.float32)


def permute_rows(block, mat):
    return jnp.einsum("no,pol->pnl", mat, block, precision=lax.Precision.HIGH)


def permute_lanes(block, mat):
    return jnp.einsum("no,pro->prn", mat, block, precision=lax.Precision.HIGH)


def cross_swap(block, m, rbits, cbits):
    def branch(k):
        def run(x):
            planes = x.shape[0]
            x = x.reshape(planes, 2 ** (rbits - k), 2**k, 2**k, 2 ** (cbits - k))
            x = jnp.transpose(x, (0, 1, 3, 2, 4))
            return x.reshape(planes, 2**rbits, 2**cbits)

        return run

    return lax.switch(m, [branch(k) for k in range(min(rbits, cbits) + 1)], block)


def plan_permute(src, rbits, cbits):
    total = rbits + cbits
    dest_of = jnp.zeros((total,), jnp.int32).at[src].set(jnp.arange(total, dtype=jnp.int32))
    pos = jnp.arange(total, dtype=jnp.int32)
    is_lane = pos < cbits
    goes_lane = dest_of < cbits
    lane_stay = is_lane & goes_lane
    lane_go = is_lane & ~goes_lane
    row_stay = ~is_lane & ~goes_lane
    row_go = ~is_lane & goes_lane
    m = jnp.sum(row_go.astype(jnp.int32))
    r_lane_stay = rank_within(dest_of, lane_stay)
    r_lane_go = rank_within(dest_of, lane_go)
    r_row_stay = rank_within(dest_of, row_stay)
    r_row_go = rank_within(dest_of, row_go)
    first_rows = jnp.where(row_go, r_row_go, m + r_row_stay)[cbits:]
    first_lanes = jnp.where(lane_go, cbits - m + r_lane_go, r_lane_stay)[:cbits]
    lane_src_pos = jnp.where(lane_stay, r_lane_stay, cbits - m + r_row_go)
    lane_members = lane_stay | row_go
    row_src_pos = jnp.where(lane_go, r_lane_go, m + r_row_stay)
    row_members = lane_go | row_stay
    second_lanes = jnp.zeros((cbits,), jnp.int32).at[
        jnp.where(lane_members, lane_src_pos, cbits)
    ].set(dest_of, mode="drop")
    second_rows = jnp.zeros((rbits,), jnp.int32).at[
        jnp.where(row_members, row_src_pos, rbits)
    ].set(dest_of - cbits, mode="drop")
    mats = (
        perm_matrix(first_rows, rbits),
        perm_matrix(first_lanes, cbits),
        perm_matrix(second_rows, rbits),
        perm_matrix(second_lanes, cbits),
    )
    return mats, m


def apply_permute(block, plan):
    (rows_a, lanes_a, rows_b, lanes_b), m = plan
    rbits = block.shape[1].bit_length() - 1
    cbits = block.shape[2].bit_length() - 1
    block = permute_rows(block, rows_a)
    block = permute_lanes(block, lanes_a)
    block = cross_swap(block, m, rbits, cbits)
    block = permute_rows(block, rows_b)
    return permute_lanes(block, lanes_b)


def make_plans(axis_order):
    nrows = lax.axis_size("rows")
    nbond = lax.axis_size("bond")
    row_devbits = nrows.bit_length() - 1
    bond_devbits = nbond.bit_length() - 1
    total_bits = ROW_BITS + COL_BITS
    lrows = ROW_BITS - row_devbits
    lcols = COL_BITS - bond_devbits
    prows = lrows - bond_devbits
    nlocal = lrows + lcols
    devbits = row_devbits + bond_devbits
    local_of = jnp.array(
        [bit if bit < nlocal else -1 for bit in range(total_bits)], dtype=jnp.int32
    )
    out_dev = [COL_BITS + lrows + k for k in range(row_devbits)] + [
        lcols + k for k in range(bond_devbits)
    ]
    dev_src = local_of[axis_order[jnp.array(out_dev, dtype=jnp.int32)]]
    pos = jnp.arange(nlocal, dtype=jnp.int32)
    is_dev = jnp.any(pos[:, None] == dev_src[None, :], axis=1)
    keep = ~is_dev
    keep_rank = rank_within(pos, keep)
    within = jnp.zeros((nlocal,), jnp.int32).at[jnp.where(keep, keep_rank, nlocal)].set(
        pos, mode="drop"
    )
    src_a = within.at[nlocal - devbits + jnp.arange(devbits)].set(dev_src)
    plan_a = plan_permute(src_a, prows, COL_BITS)
    src_dev_bits = [COL_BITS + lrows + k for k in range(row_devbits)] + [
        COL_BITS + prows + k for k in range(bond_devbits)
    ]
    pos_w = jnp.full((total_bits,), -1, jnp.int32)
    pos_w = pos_w.at[within[: nlocal - devbits]].set(jnp.arange(nlocal - devbits, dtype=jnp.int32))
    pos_w = pos_w.at[jnp.array(src_dev_bits, dtype=jnp.int32)].set(
        nlocal - devbits + jnp.arange(devbits, dtype=jnp.int32)
    )
    out_local = [b for b in range(lcols)] + [COL_BITS + k for k in range(lrows)]
    src_c = pos_w[axis_order[jnp.array(out_local, dtype=jnp.int32)]]
    plan_c = plan_permute(src_c, lrows, lcols)
    return plan_a, plan_c


def regroup(block, plans):
    plan_a, plan_c = plans
    planes = block.shape[0]
    nrows = lax.axis_size("rows")
    nbond = lax.axis_size("bond")
    lrows = 2**ROW_BITS // nrows
    lcols = 2**COL_BITS // nbond
    block = apply_permute(block, plan_a)
    block = block.reshape(planes, nrows * nbond, -1)
    block = lax.all_to_all(block, ("bond", "rows"), split_axis=1, concat_axis=1, tiled=True)
    block = block.reshape(planes, lrows, lcols)
    return apply_permute(block, plan_c)


def ring_all_gather(shard, axis):
    size = lax.axis_size(axis)
    ring = [2 * k for k in range(size // 2)] + [2 * k + 1 for k in reversed(range(size // 2))]
    pos_of = [ring.index(idx) for idx in range(size)]
    fwd = [(ring[i], ring[(i + 1) % size]) for i in range(size)]
    bwd = [(ring[(i + 1) % size], ring[i]) for i in range(size)]
    me = lax.axis_index(axis)
    my_pos = jnp.array(pos_of, dtype=jnp.int32)[me]
    ring_arr = jnp.array(ring, dtype=jnp.int32)
    planes, rows, width = shard.shape
    half = rows // 2
    ahead, behind = shard[:, :half], shard[:, half:]
    zero = jnp.int32(0)
    out = jnp.zeros((planes, size * rows, width), shard.dtype)
    out = lax.dynamic_update_slice(out, shard, (zero, me * rows, zero))
    for step in range(1, size):
        ahead = lax.ppermute(ahead, axis, fwd)
        behind = lax.ppermute(behind, axis, bwd)
        src_ahead = ring_arr[(my_pos - step) % size]
        src_behind = ring_arr[(my_pos + step) % size]
        out = lax.dynamic_update_slice(out, ahead, (zero, src_ahead * rows, zero))
        out = lax.dynamic_update_slice(out, behind, (zero, src_behind * rows + half, zero))
    return out


def ring_reduce_scatter(real_part, imag_part, axis):
    size = lax.axis_size(axis)
    ring = [2 * k for k in range(size // 2)] + [2 * k + 1 for k in reversed(range(size // 2))]
    pos_of = [ring.index(idx) for idx in range(size)]
    fwd = [(ring[i], ring[(i + 1) % size]) for i in range(size)]
    bwd = [(ring[(i + 1) % size], ring[i]) for i in range(size)]
    me = lax.axis_index(axis)
    my_pos = jnp.array(pos_of, dtype=jnp.int32)[me]
    ring_arr = jnp.array(ring, dtype=jnp.int32)
    chunk = real_part.shape[0] // size

    def part(plane, at):
        owner = ring_arr[at % size]
        return lax.dynamic_slice_in_dim(plane, owner * chunk, chunk, axis=0)

    acc_real = part(real_part, my_pos - 1)
    acc_imag = part(imag_part, my_pos + 1)
    for step in range(1, size):
        acc_real = lax.ppermute(acc_real, axis, fwd)
        acc_imag = lax.ppermute(acc_imag, axis, bwd)
        acc_real = acc_real + part(real_part, my_pos - 1 - step)
        acc_imag = acc_imag + part(imag_part, my_pos + 1 + step)
    return jnp.stack([acc_real, acc_imag])


def per_device(amps_left, amps_right, axis_order):
    plans = make_plans(axis_order)
    gathered = ring_all_gather(amps_right, "rows")
    gathered, plans = lax.optimization_barrier((gathered, plans))
    real_part = cross_dot(amps_left[0], gathered[0]) - cross_dot(amps_left[1], gathered[1])
    imag_part = cross_dot(amps_left[0], gathered[1]) + cross_dot(amps_left[1], gathered[0])
    block = ring_reduce_scatter(real_part, imag_part, "bond")
    return regroup(block, plans)


def solution(mesh):
    placed = (P(None, "rows", "bond"), P(None, "rows", "bond"), P())
    return jax.shard_map(
        per_device, mesh=mesh, in_specs=placed, out_specs=P(None, "rows", "bond"), check_vma=False
    )
```

```python
import jax
import jax.numpy as jnp
from jax import lax
from jax.sharding import PartitionSpec as P

ROW_BITS = 12
COL_BITS = 9


def cross_dot(left, right):
    return lax.dot_general(
        left,
        right,
        (((1,), (1,)), ((), ())),
        precision=lax.Precision.HIGH,
        preferred_element_type=jnp.float32,
    )


def rank_within(keys, member):
    below = (keys[None, :] < keys[:, None]) & member[None, :]
    return jnp.sum(below.astype(jnp.int32), axis=1)


def perm_matrix(new_pos, nbits):
    old = jnp.arange(2**nbits, dtype=jnp.int32)
    bits = jnp.right_shift(old[:, None], jnp.arange(nbits, dtype=jnp.int32)[None, :]) & 1
    weights = jnp.left_shift(jnp.int32(1), new_pos)
    moved = jnp.sum(bits * weights[None, :], axis=1)
    moved = lax.optimization_barrier(moved)
    return (old[:, None] == moved[None, :]).astype(jnp.float32)


def permute_rows(block, mat):
    return jnp.einsum("no,pol->pnl", mat, block, precision=lax.Precision.HIGH)


def permute_lanes(block, mat):
    return jnp.einsum("no,pro->prn", mat, block, precision=lax.Precision.HIGH)


def cross_swap(block, m, rbits, cbits):
    def branch(k):
        def run(x):
            planes = x.shape[0]
            x = x.reshape(planes, 2 ** (rbits - k), 2**k, 2**k, 2 ** (cbits - k))
            x = jnp.transpose(x, (0, 1, 3, 2, 4))
            return x.reshape(planes, 2**rbits, 2**cbits)

        return run

    return lax.switch(m, [branch(k) for k in range(min(rbits, cbits) + 1)], block)


def plan_permute(src, rbits, cbits):
    total = rbits + cbits
    dest_of = jnp.zeros((total,), jnp.int32).at[src].set(jnp.arange(total, dtype=jnp.int32))
    pos = jnp.arange(total, dtype=jnp.int32)
    is_lane = pos < cbits
    goes_lane = dest_of < cbits
    lane_stay = is_lane & goes_lane
    lane_go = is_lane & ~goes_lane
    row_stay = ~is_lane & ~goes_lane
    row_go = ~is_lane & goes_lane
    m = jnp.sum(row_go.astype(jnp.int32))
    r_lane_stay = rank_within(dest_of, lane_stay)
    r_lane_go = rank_within(dest_of, lane_go)
    r_row_stay = rank_within(dest_of, row_stay)
    r_row_go = rank_within(dest_of, row_go)
    first_rows = jnp.where(row_go, r_row_go, m + r_row_stay)[cbits:]
    first_lanes = jnp.where(lane_go, cbits - m + r_lane_go, r_lane_stay)[:cbits]
    lane_src_pos = jnp.where(lane_stay, r_lane_stay, cbits - m + r_row_go)
    lane_members = lane_stay | row_go
    row_src_pos = jnp.where(lane_go, r_lane_go, m + r_row_stay)
    row_members = lane_go | row_stay
    second_lanes = jnp.zeros((cbits,), jnp.int32).at[
        jnp.where(lane_members, lane_src_pos, cbits)
    ].set(dest_of, mode="drop")
    second_rows = jnp.zeros((rbits,), jnp.int32).at[
        jnp.where(row_members, row_src_pos, rbits)
    ].set(dest_of - cbits, mode="drop")
    mats = (
        perm_matrix(first_rows, rbits),
        perm_matrix(first_lanes, cbits),
        perm_matrix(second_rows, rbits),
        perm_matrix(second_lanes, cbits),
    )
    return mats, m


def apply_permute(block, plan):
    (rows_a, lanes_a, rows_b, lanes_b), m = plan
    rbits = block.shape[1].bit_length() - 1
    cbits = block.shape[2].bit_length() - 1
    block = permute_rows(block, rows_a)
    block = permute_lanes(block, lanes_a)
    block = cross_swap(block, m, rbits, cbits)
    block = permute_rows(block, rows_b)
    return permute_lanes(block, lanes_b)


def make_plans(axis_order):
    nrows = lax.axis_size("rows")
    nbond = lax.axis_size("bond")
    row_devbits = nrows.bit_length() - 1
    bond_devbits = nbond.bit_length() - 1
    total_bits = ROW_BITS + COL_BITS
    lrows = ROW_BITS - row_devbits
    lcols = COL_BITS - bond_devbits
    prows = lrows - bond_devbits
    nlocal = lrows + lcols
    devbits = row_devbits + bond_devbits
    local_of = jnp.array(
        [bit if bit < nlocal else -1 for bit in range(total_bits)], dtype=jnp.int32
    )
    out_dev = [COL_BITS + lrows + k for k in range(row_devbits)] + [
        lcols + k for k in range(bond_devbits)
    ]
    dev_src = local_of[axis_order[jnp.array(out_dev, dtype=jnp.int32)]]
    pos = jnp.arange(nlocal, dtype=jnp.int32)
    is_dev = jnp.any(pos[:, None] == dev_src[None, :], axis=1)
    keep = ~is_dev
    keep_rank = rank_within(pos, keep)
    within = jnp.zeros((nlocal,), jnp.int32).at[jnp.where(keep, keep_rank, nlocal)].set(
        pos, mode="drop"
    )
    src_a = within.at[nlocal - devbits + jnp.arange(devbits)].set(dev_src)
    plan_a = plan_permute(src_a, prows, COL_BITS)
    src_dev_bits = [COL_BITS + lrows + k for k in range(row_devbits)] + [
        COL_BITS + prows + k for k in range(bond_devbits)
    ]
    pos_w = jnp.full((total_bits,), -1, jnp.int32)
    pos_w = pos_w.at[within[: nlocal - devbits]].set(jnp.arange(nlocal - devbits, dtype=jnp.int32))
    pos_w = pos_w.at[jnp.array(src_dev_bits, dtype=jnp.int32)].set(
        nlocal - devbits + jnp.arange(devbits, dtype=jnp.int32)
    )
    out_local = [b for b in range(lcols)] + [COL_BITS + k for k in range(lrows)]
    src_c = pos_w[axis_order[jnp.array(out_local, dtype=jnp.int32)]]
    plan_c = plan_permute(src_c, lrows, lcols)
    return plan_a, plan_c


def regroup(block, plans):
    plan_a, plan_c = plans
    planes = block.shape[0]
    nrows = lax.axis_size("rows")
    nbond = lax.axis_size("bond")
    lrows = 2**ROW_BITS // nrows
    lcols = 2**COL_BITS // nbond
    outs = []
    for plane in range(planes):
        part = apply_permute(block[plane : plane + 1], plan_a)
        part = part.reshape(1, nrows * nbond, -1)
        part = lax.all_to_all(part, ("bond", "rows"), split_axis=1, concat_axis=1, tiled=True)
        part = part.reshape(1, lrows, lcols)
        outs.append(apply_permute(part, plan_c))
    return jnp.concatenate(outs, axis=0)


def ring_all_gather(shard, axis):
    size = lax.axis_size(axis)
    ring = [2 * k for k in range(size // 2)] + [2 * k + 1 for k in reversed(range(size // 2))]
    pos_of = [ring.index(idx) for idx in range(size)]
    fwd = [(ring[i], ring[(i + 1) % size]) for i in range(size)]
    bwd = [(ring[(i + 1) % size], ring[i]) for i in range(size)]
    me = lax.axis_index(axis)
    my_pos = jnp.array(pos_of, dtype=jnp.int32)[me]
    ring_arr = jnp.array(ring, dtype=jnp.int32)
    planes, rows, width = shard.shape
    half = rows // 2
    ahead, behind = shard[:, :half], shard[:, half:]
    zero = jnp.int32(0)
    out = jnp.zeros((planes, size * rows, width), shard.dtype)
    out = lax.dynamic_update_slice(out, shard, (zero, me * rows, zero))
    for step in range(1, size):
        ahead = lax.ppermute(ahead, axis, fwd)
        behind = lax.ppermute(behind, axis, bwd)
        src_ahead = ring_arr[(my_pos - step) % size]
        src_behind = ring_arr[(my_pos + step) % size]
        out = lax.dynamic_update_slice(out, ahead, (zero, src_ahead * rows, zero))
        out = lax.dynamic_update_slice(out, behind, (zero, src_behind * rows + half, zero))
    return out


def ring_reduce_scatter(real_part, imag_part, axis):
    size = lax.axis_size(axis)
    ring = [2 * k for k in range(size // 2)] + [2 * k + 1 for k in reversed(range(size // 2))]
    pos_of = [ring.index(idx) for idx in range(size)]
    fwd = [(ring[i], ring[(i + 1) % size]) for i in range(size)]
    bwd = [(ring[(i + 1) % size], ring[i]) for i in range(size)]
    me = lax.axis_index(axis)
    my_pos = jnp.array(pos_of, dtype=jnp.int32)[me]
    ring_arr = jnp.array(ring, dtype=jnp.int32)
    chunk = real_part.shape[0] // size

    def part(plane, at):
        owner = ring_arr[at % size]
        return lax.dynamic_slice_in_dim(plane, owner * chunk, chunk, axis=0)

    acc_real = part(real_part, my_pos - 1)
    acc_imag = part(imag_part, my_pos + 1)
    for step in range(1, size):
        acc_real = lax.ppermute(acc_real, axis, fwd)
        acc_imag = lax.ppermute(acc_imag, axis, bwd)
        acc_real = acc_real + part(real_part, my_pos - 1 - step)
        acc_imag = acc_imag + part(imag_part, my_pos + 1 + step)
    return jnp.stack([acc_real, acc_imag])


def per_device(amps_left, amps_right, axis_order):
    plans = make_plans(axis_order)
    gathered = ring_all_gather(amps_right, "rows")
    gathered, plans = lax.optimization_barrier((gathered, plans))
    real_part = cross_dot(amps_left[0], gathered[0]) - cross_dot(amps_left[1], gathered[1])
    imag_part = cross_dot(amps_left[0], gathered[1]) + cross_dot(amps_left[1], gathered[0])
    block = ring_reduce_scatter(real_part, imag_part, "bond")
    return regroup(block, plans)


def solution(mesh):
    placed = (P(None, "rows", "bond"), P(None, "rows", "bond"), P())
    return jax.shard_map(
        per_device, mesh=mesh, in_specs=placed, out_specs=P(None, "rows", "bond"), check_vma=False
    )
```

```python
import jax
import jax.numpy as jnp
from jax import lax
from jax.sharding import PartitionSpec as P

ROW_BITS = 12
COL_BITS = 9


def cross_dot(left, right):
    return lax.dot_general(
        left,
        right,
        (((1,), (1,)), ((), ())),
        precision=lax.Precision.HIGH,
        preferred_element_type=jnp.float32,
    )


def rank_within(keys, member):
    below = (keys[None, :] < keys[:, None]) & member[None, :]
    return jnp.sum(below.astype(jnp.int32), axis=1)


def perm_matrix(new_pos, nbits, order=None):
    old = jnp.arange(2**nbits, dtype=jnp.int32)
    bits = jnp.right_shift(old[:, None], jnp.arange(nbits, dtype=jnp.int32)[None, :]) & 1
    weights = jnp.left_shift(jnp.int32(1), new_pos)
    moved = jnp.sum(bits * weights[None, :], axis=1)
    if order is not None:
        moved = moved[order]
    moved = lax.optimization_barrier(moved)
    return (old[:, None] == moved[None, :]).astype(jnp.float32)


def permute_rows(block, mat):
    return jnp.einsum("no,pol->pnl", mat, block, precision=lax.Precision.HIGH)


def permute_lanes(block, mat):
    return jnp.einsum("no,pro->prn", mat, block, precision=lax.Precision.HIGH)


def cross_swap(block, m, rbits, cbits):
    def branch(k):
        def run(x):
            planes = x.shape[0]
            x = x.reshape(planes, 2 ** (rbits - k), 2**k, 2**k, 2 ** (cbits - k))
            x = jnp.transpose(x, (0, 1, 3, 2, 4))
            return x.reshape(planes, 2**rbits, 2**cbits)

        return run

    return lax.switch(m, [branch(k) for k in range(min(rbits, cbits) + 1)], block)


def plan_permute(src, rbits, cbits, lane_order=None):
    total = rbits + cbits
    dest_of = jnp.zeros((total,), jnp.int32).at[src].set(jnp.arange(total, dtype=jnp.int32))
    pos = jnp.arange(total, dtype=jnp.int32)
    is_lane = pos < cbits
    goes_lane = dest_of < cbits
    lane_stay = is_lane & goes_lane
    lane_go = is_lane & ~goes_lane
    row_stay = ~is_lane & ~goes_lane
    row_go = ~is_lane & goes_lane
    m = jnp.sum(row_go.astype(jnp.int32))
    r_lane_stay = rank_within(dest_of, lane_stay)
    r_lane_go = rank_within(dest_of, lane_go)
    r_row_stay = rank_within(dest_of, row_stay)
    r_row_go = rank_within(dest_of, row_go)
    first_rows = jnp.where(row_go, r_row_go, m + r_row_stay)[cbits:]
    first_lanes = jnp.where(lane_go, cbits - m + r_lane_go, r_lane_stay)[:cbits]
    lane_src_pos = jnp.where(lane_stay, r_lane_stay, cbits - m + r_row_go)
    lane_members = lane_stay | row_go
    row_src_pos = jnp.where(lane_go, r_lane_go, m + r_row_stay)
    row_members = lane_go | row_stay
    second_lanes = jnp.zeros((cbits,), jnp.int32).at[
        jnp.where(lane_members, lane_src_pos, cbits)
    ].set(dest_of, mode="drop")
    second_rows = jnp.zeros((rbits,), jnp.int32).at[
        jnp.where(row_members, row_src_pos, rbits)
    ].set(dest_of - cbits, mode="drop")
    mats = (
        perm_matrix(first_rows, rbits),
        perm_matrix(first_lanes, cbits, lane_order),
        perm_matrix(second_rows, rbits),
        perm_matrix(second_lanes, cbits),
    )
    return mats, m


def apply_permute(block, plan):
    (rows_a, lanes_a, rows_b, lanes_b), m = plan
    rbits = block.shape[1].bit_length() - 1
    cbits = block.shape[2].bit_length() - 1
    block = permute_rows(block, rows_a)
    block = permute_lanes(block, lanes_a)
    block = cross_swap(block, m, rbits, cbits)
    block = permute_rows(block, rows_b)
    return permute_lanes(block, lanes_b)


def make_plans(axis_order, lane_order):
    nrows = lax.axis_size("rows")
    nbond = lax.axis_size("bond")
    row_devbits = nrows.bit_length() - 1
    bond_devbits = nbond.bit_length() - 1
    total_bits = ROW_BITS + COL_BITS
    lrows = ROW_BITS - row_devbits
    lcols = COL_BITS - bond_devbits
    prows = lrows - bond_devbits
    nlocal = lrows + lcols
    devbits = row_devbits + bond_devbits
    local_of = jnp.array(
        [bit if bit < nlocal else -1 for bit in range(total_bits)], dtype=jnp.int32
    )
    out_dev = [COL_BITS + lrows + k for k in range(row_devbits)] + [
        lcols + k for k in range(bond_devbits)
    ]
    dev_src = local_of[axis_order[jnp.array(out_dev, dtype=jnp.int32)]]
    pos = jnp.arange(nlocal, dtype=jnp.int32)
    is_dev = jnp.any(pos[:, None] == dev_src[None, :], axis=1)
    keep = ~is_dev
    keep_rank = rank_within(pos, keep)
    within = jnp.zeros((nlocal,), jnp.int32).at[jnp.where(keep, keep_rank, nlocal)].set(
        pos, mode="drop"
    )
    src_a = within.at[nlocal - devbits + jnp.arange(devbits)].set(dev_src)
    plan_a = plan_permute(src_a, prows, COL_BITS, lane_order)
    src_dev_bits = [COL_BITS + lrows + k for k in range(row_devbits)] + [
        COL_BITS + prows + k for k in range(bond_devbits)
    ]
    pos_w = jnp.full((total_bits,), -1, jnp.int32)
    pos_w = pos_w.at[within[: nlocal - devbits]].set(jnp.arange(nlocal - devbits, dtype=jnp.int32))
    pos_w = pos_w.at[jnp.array(src_dev_bits, dtype=jnp.int32)].set(
        nlocal - devbits + jnp.arange(devbits, dtype=jnp.int32)
    )
    out_local = [b for b in range(lcols)] + [COL_BITS + k for k in range(lrows)]
    src_c = pos_w[axis_order[jnp.array(out_local, dtype=jnp.int32)]]
    plan_c = plan_permute(src_c, lrows, lcols)
    return plan_a, plan_c


def regroup(block, plans):
    plan_a, plan_c = plans
    planes = block.shape[0]
    nrows = lax.axis_size("rows")
    nbond = lax.axis_size("bond")
    lrows = 2**ROW_BITS // nrows
    lcols = 2**COL_BITS // nbond
    block = apply_permute(block, plan_a)
    block = block.reshape(planes, nrows * nbond, -1)
    block = lax.all_to_all(block, ("bond", "rows"), split_axis=1, concat_axis=1, tiled=True)
    block = block.reshape(planes, lrows, lcols)
    return apply_permute(block, plan_c)


def ring_all_gather(shard, axis):
    size = lax.axis_size(axis)
    ring = [2 * k for k in range(size // 2)] + [2 * k + 1 for k in reversed(range(size // 2))]
    pos_of = [ring.index(idx) for idx in range(size)]
    fwd = [(ring[i], ring[(i + 1) % size]) for i in range(size)]
    bwd = [(ring[(i + 1) % size], ring[i]) for i in range(size)]
    me = lax.axis_index(axis)
    my_pos = jnp.array(pos_of, dtype=jnp.int32)[me]
    ring_arr = jnp.array(ring, dtype=jnp.int32)
    rows = shard.shape[1]
    half = rows // 2
    ahead, behind = shard[:, :half], shard[:, half:]
    pieces = [[shard]]
    order = [me * rows + jnp.arange(rows, dtype=jnp.int32)]
    for step in range(1, size):
        ahead = lax.ppermute(ahead, axis, fwd)
        behind = lax.ppermute(behind, axis, bwd)
        pieces.append([ahead, behind])
        src_ahead = ring_arr[(my_pos - step) % size]
        src_behind = ring_arr[(my_pos + step) % size]
        order.append(src_ahead * rows + jnp.arange(half, dtype=jnp.int32))
        order.append(src_behind * rows + half + jnp.arange(half, dtype=jnp.int32))
    return pieces, jnp.concatenate(order)


def ring_reduce_scatter(real_part, imag_part, axis):
    size = lax.axis_size(axis)
    ring = [2 * k for k in range(size // 2)] + [2 * k + 1 for k in reversed(range(size // 2))]
    pos_of = [ring.index(idx) for idx in range(size)]
    fwd = [(ring[i], ring[(i + 1) % size]) for i in range(size)]
    bwd = [(ring[(i + 1) % size], ring[i]) for i in range(size)]
    me = lax.axis_index(axis)
    my_pos = jnp.array(pos_of, dtype=jnp.int32)[me]
    ring_arr = jnp.array(ring, dtype=jnp.int32)
    chunk = real_part.shape[0] // size

    def part(plane, at):
        owner = ring_arr[at % size]
        return lax.dynamic_slice_in_dim(plane, owner * chunk, chunk, axis=0)

    acc_real = part(real_part, my_pos - 1)
    acc_imag = part(imag_part, my_pos + 1)
    for step in range(1, size):
        acc_real = lax.ppermute(acc_real, axis, fwd)
        acc_imag = lax.ppermute(acc_imag, axis, bwd)
        acc_real = acc_real + part(real_part, my_pos - 1 - step)
        acc_imag = acc_imag + part(imag_part, my_pos + 1 + step)
    return jnp.stack([acc_real, acc_imag])


def per_device(amps_left, amps_right, axis_order):
    pieces, lane_order = ring_all_gather(amps_right, "rows")
    plans = make_plans(axis_order, lane_order)
    steps = len(pieces)
    cuts = sorted({0, max(steps - 3, 1), max(steps - 1, 1), steps})
    real_cols, imag_cols = [], []
    for first, stop in zip(cuts[:-1], cuts[1:]):
        group = jnp.concatenate([p for step in pieces[first:stop] for p in step], axis=1)
        if first == 0:
            group, plans = lax.optimization_barrier((group, plans))
        real_cols.append(
            cross_dot(amps_left[0], group[0]) - cross_dot(amps_left[1], group[1])
        )
        imag_cols.append(
            cross_dot(amps_left[0], group[1]) + cross_dot(amps_left[1], group[0])
        )
    real_part = jnp.concatenate(real_cols, axis=1)
    imag_part = jnp.concatenate(imag_cols, axis=1)
    block = ring_reduce_scatter(real_part, imag_part, "bond")
    return regroup(block, plans)


def solution(mesh):
    placed = (P(None, "rows", "bond"), P(None, "rows", "bond"), P())
    return jax.shard_map(
        per_device, mesh=mesh, in_specs=placed, out_specs=P(None, "rows", "bond"), check_vma=False
    )
```

```python
import jax
import jax.numpy as jnp
from jax import lax
from jax.sharding import PartitionSpec as P

ROW_BITS = 12
COL_BITS = 9


def cross_dot(left, right):
    return lax.dot_general(
        left,
        right,
        (((1,), (1,)), ((), ())),
        precision=lax.Precision.HIGH,
        preferred_element_type=jnp.float32,
    )


def rank_within(keys, member):
    below = (keys[None, :] < keys[:, None]) & member[None, :]
    return jnp.sum(below.astype(jnp.int32), axis=1)


def perm_matrix(new_pos, nbits):
    old = jnp.arange(2**nbits, dtype=jnp.int32)
    bits = jnp.right_shift(old[:, None], jnp.arange(nbits, dtype=jnp.int32)[None, :]) & 1
    weights = jnp.left_shift(jnp.int32(1), new_pos)
    moved = jnp.sum(bits * weights[None, :], axis=1)
    moved = lax.optimization_barrier(moved)
    return (old[:, None] == moved[None, :]).astype(jnp.float32)


def permute_rows(block, mat):
    return jnp.einsum("no,pol->pnl", mat, block, precision=lax.Precision.HIGH)


def permute_lanes(block, mat):
    return jnp.einsum("no,pro->prn", mat, block, precision=lax.Precision.HIGH)


def cross_swap(block, m, rbits, cbits):
    def branch(k):
        def run(x):
            planes = x.shape[0]
            x = x.reshape(planes, 2 ** (rbits - k), 2**k, 2**k, 2 ** (cbits - k))
            x = jnp.transpose(x, (0, 1, 3, 2, 4))
            return x.reshape(planes, 2**rbits, 2**cbits)

        return run

    return lax.switch(m, [branch(k) for k in range(min(rbits, cbits) + 1)], block)


def plan_permute(src, rbits, cbits):
    total = rbits + cbits
    dest_of = jnp.zeros((total,), jnp.int32).at[src].set(jnp.arange(total, dtype=jnp.int32))
    pos = jnp.arange(total, dtype=jnp.int32)
    is_lane = pos < cbits
    goes_lane = dest_of < cbits
    lane_stay = is_lane & goes_lane
    lane_go = is_lane & ~goes_lane
    row_stay = ~is_lane & ~goes_lane
    row_go = ~is_lane & goes_lane
    m = jnp.sum(row_go.astype(jnp.int32))
    r_lane_stay = rank_within(dest_of, lane_stay)
    r_lane_go = rank_within(dest_of, lane_go)
    r_row_stay = rank_within(dest_of, row_stay)
    r_row_go = rank_within(dest_of, row_go)
    first_rows = jnp.where(row_go, r_row_go, m + r_row_stay)[cbits:]
    first_lanes = jnp.where(lane_go, cbits - m + r_lane_go, r_lane_stay)[:cbits]
    lane_src_pos = jnp.where(lane_stay, r_lane_stay, cbits - m + r_row_go)
    lane_members = lane_stay | row_go
    row_src_pos = jnp.where(lane_go, r_lane_go, m + r_row_stay)
    row_members = lane_go | row_stay
    second_lanes = jnp.zeros((cbits,), jnp.int32).at[
        jnp.where(lane_members, lane_src_pos, cbits)
    ].set(dest_of, mode="drop")
    second_rows = jnp.zeros((rbits,), jnp.int32).at[
        jnp.where(row_members, row_src_pos, rbits)
    ].set(dest_of - cbits, mode="drop")
    mats = (
        perm_matrix(first_rows, rbits),
        perm_matrix(first_lanes, cbits),
        perm_matrix(second_rows, rbits),
        perm_matrix(second_lanes, cbits),
    )
    return mats, m


def apply_permute(block, plan):
    (rows_a, lanes_a, rows_b, lanes_b), m = plan
    rbits = block.shape[1].bit_length() - 1
    cbits = block.shape[2].bit_length() - 1
    block = permute_rows(block, rows_a)
    block = permute_lanes(block, lanes_a)
    block = cross_swap(block, m, rbits, cbits)
    block = permute_rows(block, rows_b)
    return permute_lanes(block, lanes_b)


def make_plans(axis_order):
    nrows = lax.axis_size("rows")
    nbond = lax.axis_size("bond")
    row_devbits = nrows.bit_length() - 1
    bond_devbits = nbond.bit_length() - 1
    total_bits = ROW_BITS + COL_BITS
    lrows = ROW_BITS - row_devbits
    lcols = COL_BITS - bond_devbits
    prows = lrows - bond_devbits
    nlocal = lrows + lcols
    devbits = row_devbits + bond_devbits
    local_of = jnp.array(
        [bit if bit < nlocal else -1 for bit in range(total_bits)], dtype=jnp.int32
    )
    out_dev = [COL_BITS + lrows + k for k in range(row_devbits)] + [
        lcols + k for k in range(bond_devbits)
    ]
    dev_src = local_of[axis_order[jnp.array(out_dev, dtype=jnp.int32)]]
    pos = jnp.arange(nlocal, dtype=jnp.int32)
    is_dev = jnp.any(pos[:, None] == dev_src[None, :], axis=1)
    keep = ~is_dev
    out_local = [b for b in range(lcols)] + [COL_BITS + k for k in range(lrows)]
    dest_out = jnp.zeros((total_bits,), jnp.int32).at[
        axis_order[jnp.array(out_local, dtype=jnp.int32)]
    ].set(jnp.arange(nlocal, dtype=jnp.int32))
    keep_rank = rank_within(dest_out[:nlocal], keep)
    within = jnp.zeros((nlocal,), jnp.int32).at[jnp.where(keep, keep_rank, nlocal)].set(
        pos, mode="drop"
    )
    src_a = within.at[nlocal - devbits + jnp.arange(devbits)].set(dev_src)
    plan_a = plan_permute(src_a, prows, COL_BITS)
    src_dev_bits = [COL_BITS + lrows + k for k in range(row_devbits)] + [
        COL_BITS + prows + k for k in range(bond_devbits)
    ]
    pos_w = jnp.full((total_bits,), -1, jnp.int32)
    pos_w = pos_w.at[within[: nlocal - devbits]].set(jnp.arange(nlocal - devbits, dtype=jnp.int32))
    pos_w = pos_w.at[jnp.array(src_dev_bits, dtype=jnp.int32)].set(
        nlocal - devbits + jnp.arange(devbits, dtype=jnp.int32)
    )
    src_c = pos_w[axis_order[jnp.array(out_local, dtype=jnp.int32)]]
    plan_c = plan_permute(src_c, lrows, lcols)
    return plan_a, plan_c


def regroup(block, plans):
    plan_a, plan_c = plans
    planes = block.shape[0]
    nrows = lax.axis_size("rows")
    nbond = lax.axis_size("bond")
    lrows = 2**ROW_BITS // nrows
    lcols = 2**COL_BITS // nbond
    block = apply_permute(block, plan_a)
    block = block.reshape(planes, nrows * nbond, -1)
    block = lax.all_to_all(block, ("bond", "rows"), split_axis=1, concat_axis=1, tiled=True)
    block = block.reshape(planes, lrows, lcols)
    return apply_permute(block, plan_c)


def ring_all_gather(shard, axis):
    size = lax.axis_size(axis)
    ring = [2 * k for k in range(size // 2)] + [2 * k + 1 for k in reversed(range(size // 2))]
    pos_of = [ring.index(idx) for idx in range(size)]
    fwd = [(ring[i], ring[(i + 1) % size]) for i in range(size)]
    bwd = [(ring[(i + 1) % size], ring[i]) for i in range(size)]
    me = lax.axis_index(axis)
    my_pos = jnp.array(pos_of, dtype=jnp.int32)[me]
    ring_arr = jnp.array(ring, dtype=jnp.int32)
    planes, rows, width = shard.shape
    half = rows // 2
    ahead, behind = shard[:, :half], shard[:, half:]
    zero = jnp.int32(0)
    out = jnp.zeros((planes, size * rows, width), shard.dtype)
    out = lax.dynamic_update_slice(out, shard, (zero, me * rows, zero))
    for step in range(1, size):
        ahead = lax.ppermute(ahead, axis, fwd)
        behind = lax.ppermute(behind, axis, bwd)
        src_ahead = ring_arr[(my_pos - step) % size]
        src_behind = ring_arr[(my_pos + step) % size]
        out = lax.dynamic_update_slice(out, ahead, (zero, src_ahead * rows, zero))
        out = lax.dynamic_update_slice(out, behind, (zero, src_behind * rows + half, zero))
    return out


def ring_reduce_scatter(real_part, imag_part, axis):
    size = lax.axis_size(axis)
    ring = [2 * k for k in range(size // 2)] + [2 * k + 1 for k in reversed(range(size // 2))]
    pos_of = [ring.index(idx) for idx in range(size)]
    fwd = [(ring[i], ring[(i + 1) % size]) for i in range(size)]
    bwd = [(ring[(i + 1) % size], ring[i]) for i in range(size)]
    me = lax.axis_index(axis)
    my_pos = jnp.array(pos_of, dtype=jnp.int32)[me]
    ring_arr = jnp.array(ring, dtype=jnp.int32)
    chunk = real_part.shape[0] // size

    def part(plane, at):
        owner = ring_arr[at % size]
        return lax.dynamic_slice_in_dim(plane, owner * chunk, chunk, axis=0)

    acc_real = part(real_part, my_pos - 1)
    acc_imag = part(imag_part, my_pos + 1)
    for step in range(1, size):
        acc_real = lax.ppermute(acc_real, axis, fwd)
        acc_imag = lax.ppermute(acc_imag, axis, bwd)
        acc_real = acc_real + part(real_part, my_pos - 1 - step)
        acc_imag = acc_imag + part(imag_part, my_pos + 1 + step)
    return jnp.stack([acc_real, acc_imag])


def per_device(amps_left, amps_right, axis_order):
    plans = make_plans(axis_order)
    gathered = ring_all_gather(amps_right, "rows")
    gathered, plans = lax.optimization_barrier((gathered, plans))
    real_part = cross_dot(amps_left[0], gathered[0]) - cross_dot(amps_left[1], gathered[1])
    imag_part = cross_dot(amps_left[0], gathered[1]) + cross_dot(amps_left[1], gathered[0])
    block = ring_reduce_scatter(real_part, imag_part, "bond")
    return regroup(block, plans)


def solution(mesh):
    placed = (P(None, "rows", "bond"), P(None, "rows", "bond"), P())
    return jax.shard_map(
        per_device, mesh=mesh, in_specs=placed, out_specs=P(None, "rows", "bond"), check_vma=False
    )
```
